128 devices in a mesh: oy: 8 (over x, core), ox: 16 (over y, z).
Axes of the slice: x: 4, y: 4, z: 4, core: 2. Of those that a mesh axis runs over, the one named last changes fastest.
Arguments:
- atm_flux: float32 [8, 256, 1024], P(None, ('oy', 'ox')), may hold values from -6 to 6
- remap_index: int32 [4, 512, 4096], P(None, 'oy', 'ox'), may hold values from 0 to 2447, as said below
- remap_weight: float32 [4, 512, 4096], P(None, 'oy', 'ox'), may hold values from 0.1 to 1
- coupling: float32 [2, 8], replicated, may hold values from -0.3 to 0.3
- land_mask: int32 [512, 4096], P('oy', 'ox'), may hold values 0 or 1
- tracers: float32 [2, 16, 512, 4096], P(None, None, 'oy', 'ox'), may hold values from -6 to 6
- u_vel: bfloat16 [16, 512, 4096], P(None, 'oy', 'ox'), may hold values from -0.23925781 to 0.23925781
- v_vel: bfloat16 [16, 512, 4096], P(None, 'oy', 'ox'), may hold values from -0.23925781 to 0.23925781
Outputs:
- ocean_flux: float32 [8, 512, 4096], P(None, 'oy', 'ox')
- new_tracers: float32 [2, 16, 512, 4096], P(None, None, 'oy', 'ox')
The draws below stay inside these ranges and needn't reach their ends.
Inputs may be any that keep to these rules, and one draw needn't show every extreme that they name: `remap_index`: each index lies within 2 rows and 2 columns of the atmosphere cell below its ocean cell in the tile's block padded by 2 on each side, flattened row by row with 68 per row.
All inputs are finite; a program needn't handle non-finite values. No bound on the sum of `land_mask` on one device may be relied on, other than what follows from the above.
Results may differ from the reference program's by a relative error of at most 0.0003.
Values sent between devices are 32-bit elements; how exact they have to be, the bound alone decides.
No kernel may reach another device: no remote copies, remote signals or barrier semaphores. Data moves between devices by JAX's collectives and lax.ppermute only.
A program may use at most 128 MiB of HBM per device.

```python
import math
import jax
import jax.numpy as jnp
from jax import lax

NF = 8
LEV = 16
K = 4
H = 2
STEPS = 8
OR = 64
OC = 256
AC = 64
AR = 32
ALAT = 256
ALON = 1024
NOR = 512
NOC = 4096


def draw_remap_index(key, part):
    first, second = jax.random.split(key)
    shape = (K, NOR, NOC)
    row_off = jax.random.randint(first, shape, -H, H + 1)
    col_off = jax.random.randint(second, shape, -H, H + 1)
    rows = (jnp.arange(NOR, dtype=jnp.int32) % OR)[None, :, None]
    cols = (jnp.arange(NOC, dtype=jnp.int32) % OC)[None, None, :]
    leading = (jnp.arange(K, dtype=jnp.int32) == 0)[:, None, None]
    upper = leading & (rows == OR - 1) & (cols == OC - 1)
    lower = leading & (rows == 0) & (cols == 0)
    row_off = jnp.where(upper, H, jnp.where(lower, -H, row_off))
    col_off = jnp.where(upper, H, jnp.where(lower, -H, col_off))
    base_row = rows * (AR - 1) // (OR - 1) + H
    base_col = cols * (AC - 1) // (OC - 1) + H
    return ((base_row + row_off) * (AC + 2 * H) + base_col + col_off).astype(jnp.int32)


def set_ends(values, stream_key, smallest, largest):
    index_at = [jax.random.randint(jax.random.fold_in(stream_key, axis), (), 0, length) for axis, length in enumerate(values.shape)]
    longest = values.shape.index(max(values.shape))
    beside = index_at[:longest] + [(index_at[longest] + 1) % values.shape[longest]] + index_at[longest + 1:]
    return values.at[tuple(index_at)].set(smallest).at[tuple(beside)].set(largest)


def shard_levels(stream_key, shape, cuts, smallest, top_value):
    factor_of, own = 1.0, jax.random.fold_in(stream_key, 6)
    for axis_at, blocks in cuts:
        draws = jnp.exp(jax.random.uniform(jax.random.fold_in(own, axis_at), (blocks,), jnp.float32, smallest / len(cuts), top_value / len(cuts)))
        factor_of = factor_of * jnp.repeat(draws, shape[axis_at] // blocks).reshape([-1 if axis == axis_at else 1 for axis in range(len(shape))])
    return factor_of


def gaussian(own_key, extent, scale, reach, shards=(), held_as=jnp.bfloat16):
    gain = shard_levels(own_key, extent, shards, -0.22, 0.18) if shards else 1.0
    drawn = jax.random.normal(own_key, extent, jnp.float32) * scale * gain
    return jnp.minimum(jnp.maximum(drawn, -reach), reach).astype(held_as)


def setup_inputs(seed: int = 0) -> dict:
    splits = jax.random.split(jax.random.key(seed), 9)
    atm_flux = gaussian(splits[0], (NF, ALAT, ALON), 1.0, 6.0, ((1, 128),), jnp.float32)
    remap_index = draw_remap_index(jax.random.fold_in(splits[8], 71), 0)
    remap_weight = jnp.clip(jnp.exp(math.log(1.0) - 2.3025851 * jax.random.uniform(splits[2], (K, NOR, NOC), jnp.float32) ** shard_levels(splits[2], (K, NOR, NOC), ((1, 8), (2, 16)), -0.2, 0.2)), 0.1, 1.0)
    coupling = gaussian(splits[3], (2, NF), 0.05, 0.3, (), jnp.float32)
    land_mask = set_ends((jax.random.randint(splits[4], (NOR, NOC), 0, 4) < 3).astype(jnp.int32), jax.random.fold_in(splits[4], 1), 0, 1)
    tracers = gaussian(splits[5], (2, LEV, NOR, NOC), 1.0, 6.0, ((2, 8), (3, 16)), jnp.float32)
    u_vel = jnp.clip(jax.random.uniform(splits[6], (LEV, NOR, NOC), jnp.float32, -0.23925781, 0.23925781) * shard_levels(splits[6], (LEV, NOR, NOC), ((1, 8), (2, 16)), -0.4, 0.0), -0.23925781, 0.23925781).astype(jnp.bfloat16)
    v_vel = jnp.clip(jax.random.uniform(splits[7], (LEV, NOR, NOC), jnp.float32, -0.23925781, 0.23925781) * shard_levels(splits[7], (LEV, NOR, NOC), ((1, 8), (2, 16)), -0.4, 0.0), -0.23925781, 0.23925781).astype(jnp.bfloat16)
    return {"atm_flux": atm_flux, "remap_index": remap_index, "remap_weight": remap_weight, "coupling": coupling, "land_mask": land_mask, "tracers": tracers, "u_vel": u_vel, "v_vel": v_vel}


def tendency(state, west, east, south, north, u_flow, v_flow):
    above = jnp.concatenate([state[..., :1, :, :], state[..., :-1, :, :]], axis=-3)
    below = jnp.concatenate([state[..., 1:, :, :], state[..., -1:, :, :]], axis=-3)
    total = -jnp.maximum(u_flow, 0.0) * (state - west) - jnp.minimum(u_flow, 0.0) * (east - state)
    total = total - jnp.maximum(v_flow, 0.0) * (state - south) - jnp.minimum(v_flow, 0.0) * (north - state)
    total = total + 0.08 * (west + east + south + north - 4.0 * state)
    return total + 0.08 * (above + below - 2.0 * state)


def evolve(state, force, mask_f, u_flow, v_flow):
    fold_cols = ((NOC // 2 + OC - 1 - jnp.arange(NOC, dtype=jnp.int32)) % NOC).astype(jnp.int32)
    for step_num in range(STEPS):
        west = jnp.roll(state, 1, axis=2)
        east = jnp.roll(state, -1, axis=2)
        south = jnp.concatenate([jnp.zeros_like(state[:, :1, :]), state[:, :-1, :]], axis=1)
        folded = jnp.take(state[:, -1:, :], fold_cols, axis=2)
        north = jnp.concatenate([state[:, 1:, :], folded], axis=1)
        tend = tendency(state, west, east, south, north, u_flow, v_flow)
        tend = tend.at[0].add(force)
        state = state + mask_f * tend
    return state


def reference(atm_flux, remap_index, remap_weight, coupling, land_mask, tracers, u_vel, v_vel):
    pad_lat = jnp.pad(atm_flux, ((0, 0), (H, H), (0, 0)))
    padded = jnp.concatenate([pad_lat[..., -H:], pad_lat, pad_lat[..., :H]], axis=2)
    width = ALON + 2 * H
    flat = padded.reshape(NF, -1)
    tile_rows = (jnp.arange(NOR, dtype=jnp.int32) // OR)[:, None]
    tile_cols = (jnp.arange(NOC, dtype=jnp.int32) // OC)[None, :]
    ocean_flux = jnp.zeros((NF, NOR, NOC), jnp.float32)
    for source in range(K):
        index = remap_index[source]
        grow = tile_rows * AR + index // (AC + 2 * H)
        gcol = tile_cols * AC + index % (AC + 2 * H)
        picked = jnp.take(flat, (grow * width + gcol).astype(jnp.int32), axis=1)
        ocean_flux = ocean_flux + remap_weight[source][None] * picked
    forcing = jnp.einsum("tf,frc->trc", coupling, ocean_flux, precision=lax.Precision.HIGHEST)
    mask_f = land_mask.astype(jnp.float32)
    u_flow = u_vel.astype(jnp.float32)
    v_flow = v_vel.astype(jnp.float32)
    new_tracers = lax.map(lambda pair: evolve(pair[0], pair[1], mask_f, u_flow, v_flow), (tracers, forcing))
    return ocean_flux, new_tracers
```

```python
import jax
import jax.numpy as jnp
from jax import lax
from jax.sharding import PartitionSpec as P

H = 2
STEPS = 8
WIDE = 8
LANES = 384
HIGH = lax.Precision.HIGHEST


def with_halo(cells, sides, width, closed):
    for axis, dim in sides:
        count = lax.axis_size(axis)
        ends = count if closed else count - 1
        head = lax.slice_in_dim(cells, 0, width, axis=dim)
        tail = lax.slice_in_dim(cells, cells.shape[dim] - width, cells.shape[dim], axis=dim)
        cells = jnp.concatenate(
            [
                lax.ppermute(tail, axis, [(i, (i + 1) % count) for i in range(ends)]),
                cells,
                lax.ppermute(head, axis, [((i + 1) % count, i) for i in range(ends)]),
            ],
            axis=dim,
        )
    return cells


def tendency(state, west, east, south, north, u_flow, v_flow):
    above = jnp.concatenate([state[..., :1, :, :], state[..., :-1, :, :]], axis=-3)
    below = jnp.concatenate([state[..., 1:, :, :], state[..., -1:, :, :]], axis=-3)
    total = -jnp.maximum(u_flow, 0.0) * (state - west) - jnp.minimum(u_flow, 0.0) * (east - state)
    total = (
        total
        - jnp.maximum(v_flow, 0.0) * (state - south)
        - jnp.minimum(v_flow, 0.0) * (north - state)
    )
    total = total + 0.08 * (west + east + south + north - 4.0 * state)
    return total + 0.08 * (above + below - 2.0 * state)


def extend_rows(blocks, flips):
    rows_n = lax.axis_size("oy")
    cols_n = lax.axis_size("ox")
    on_top = lax.axis_index("oy") == rows_n - 1
    tops = [b[..., -WIDE:, :] for b in blocks]
    bots = [b[..., :WIDE, :] for b in blocks]
    south = lax.ppermute(tops, "oy", [(i, i + 1) for i in range(rows_n - 1)])
    north = lax.ppermute(bots, "oy", [(i + 1, i) for i in range(rows_n - 1)])
    top_row = (rows_n - 1) * cols_n
    fold = lax.ppermute(
        tops,
        ("oy", "ox"),
        [(top_row + (cols_n // 2 - j) % cols_n, top_row + j) for j in range(cols_n)],
    )
    out = []
    for b, s, n, f, neg in zip(blocks, south, north, fold, flips):
        ghost = f[..., ::-1, ::-1]
        if neg:
            ghost = -ghost
        n = jnp.where(on_top, ghost, n)
        out.append(jnp.concatenate([b, n, s], axis=-2))
    return out


def extend_cols(blocks):
    cols_n = lax.axis_size("ox")
    easts = [b[..., -WIDE:] for b in blocks]
    wests = [b[..., :WIDE] for b in blocks]
    from_w = lax.ppermute(easts, "ox", [(i, (i + 1) % cols_n) for i in range(cols_n)])
    from_e = lax.ppermute(wests, "ox", [((i + 1) % cols_n, i) for i in range(cols_n)])
    out = []
    for b, w, e in zip(blocks, from_w, from_e):
        gap = jnp.zeros(b.shape[:-1] + (LANES - b.shape[-1] - 2 * WIDE,), b.dtype)
        out.append(jnp.concatenate([b, e, gap, w], axis=-1))
    return out


def extend(blocks, flips):
    return extend_cols(extend_rows(blocks, flips))


def remap(padded, remap_index, remap_weight):
    nf, arows, acols = padded.shape
    kk, orows, ocols = remap_index.shape
    base_r = jnp.arange(orows, dtype=jnp.int32) * (arows - 2 * H - 1) // (orows - 1) + H
    base_c = jnp.arange(ocols, dtype=jnp.int32) * (acols - 2 * H - 1) // (ocols - 1) + H
    offs = jnp.arange(2 * H + 1, dtype=jnp.int32) - H
    pick_r = (
        (base_r[None, :, None] + offs[:, None, None])
        == jnp.arange(arows, dtype=jnp.int32)[None, None, :]
    ).astype(jnp.float32).reshape(-1, arows)
    pick_c = (
        jnp.arange(acols, dtype=jnp.int32)[:, None, None]
        == (base_c[None, None, :] + offs[None, :, None])
    ).astype(jnp.float32).reshape(acols, -1)
    lifted = jnp.einsum("pa,fab->fpb", pick_r, padded, precision=HIGH)
    window = jnp.einsum("fpb,bq->fpq", lifted, pick_c, precision=HIGH)
    window = window.reshape(nf, 2 * H + 1, orows, 2 * H + 1, ocols)
    row_of = remap_index // acols - base_r[None, :, None] + H
    col_of = remap_index % acols - base_c[None, None, :] + H
    inside = (row_of >= 0) & (row_of <= 2 * H) & (col_of >= 0) & (col_of <= 2 * H)
    slot = jnp.where(inside, row_of * (2 * H + 1) + col_of, -1)
    slots = jnp.arange((2 * H + 1) ** 2, dtype=jnp.int32)
    wsum = jnp.sum(
        jnp.where(slot[:, None] == slots[None, :, None, None], remap_weight[:, None], 0.0),
        axis=0,
    ).reshape(2 * H + 1, 2 * H + 1, orows, ocols)
    fast = jnp.sum(window * wsum.transpose(0, 2, 1, 3)[None], axis=(1, 3))
    missed = jnp.logical_not(jnp.all(inside))

    def general():
        flat = padded.reshape(nf, -1)
        total = jnp.zeros((nf,) + remap_index.shape[1:], jnp.float32)
        for source in range(kk):
            picked = jnp.take(flat, remap_index[source], axis=1)
            total = total + remap_weight[source][None] * picked
        return total

    return lax.cond(missed, general, lambda: fast)


def on_device(atm_flux, remap_index, remap_weight, coupling, land_mask, tracers, u_vel, v_vel):
    mask_f = land_mask.astype(jnp.float32)
    u_flow = u_vel.astype(jnp.float32)
    v_flow = v_vel.astype(jnp.float32)
    state, u_x, v_x, m_x = extend([tracers, u_flow, v_flow, mask_f], [False, True, True, False])

    atm_tile = lax.all_to_all(atm_flux, "ox", split_axis=2, concat_axis=1, tiled=True)
    lon_wide = with_halo(atm_tile, (("ox", 2),), H, True)
    padded = with_halo(lon_wide, (("oy", 1),), H, False)
    ocean_flux = remap(padded, remap_index, remap_weight)
    forcing = jnp.einsum("tf,frc->trc", coupling, ocean_flux, precision=HIGH)
    (f_x,) = extend([forcing], [False])

    def advance(step_num, s):
        west = jnp.roll(s, 1, axis=-1)
        east = jnp.roll(s, -1, axis=-1)
        south = jnp.roll(s, 1, axis=-2)
        north = jnp.roll(s, -1, axis=-2)
        tend = tendency(s, west, east, south, north, u_x, v_x)
        tend = tend.at[:, 0].add(f_x)
        return s + m_x * tend

    final = lax.fori_loop(0, STEPS, advance, state)
    rows, cols = tracers.shape[-2:]
    return (ocean_flux, final[..., :rows, :cols])


def solution(mesh):
    placed = (
        P(None, ("oy", "ox"), None),
        P(None, "oy", "ox"),
        P(None, "oy", "ox"),
        P(),
        P("oy", "ox"),
        P(None, None, "oy", "ox"),
        P(None, "oy", "ox"),
        P(None, "oy", "ox"),
    )
    return jax.shard_map(
        on_device,
        mesh=mesh,
        in_specs=placed,
        out_specs=(P(None, "oy", "ox"), P(None, None, "oy", "ox")),
        check_vma=False,
    )
```

```python
import jax
import jax.numpy as jnp
from jax import lax
from jax.sharding import PartitionSpec as P
from jax.experimental import pallas as pl
from jax.experimental.pallas import tpu as pltpu

H = 2
STEPS = 8
WIDE = 8
LANES = 384
HIGH = lax.Precision.HIGHEST


def with_halo(cells, sides, width, closed):
    for axis, dim in sides:
        count = lax.axis_size(axis)
        ends = count if closed else count - 1
        head = lax.slice_in_dim(cells, 0, width, axis=dim)
        tail = lax.slice_in_dim(cells, cells.shape[dim] - width, cells.shape[dim], axis=dim)
        cells = jnp.concatenate(
            [
                lax.ppermute(tail, axis, [(i, (i + 1) % count) for i in range(ends)]),
                cells,
                lax.ppermute(head, axis, [((i + 1) % count, i) for i in range(ends)]),
            ],
            axis=dim,
        )
    return cells


def extend(blocks, flips):
    rows_n = lax.axis_size("oy")
    cols_n = lax.axis_size("ox")
    on_top = lax.axis_index("oy") == rows_n - 1
    sizes = [b.shape[0] for b in blocks]
    sign = jnp.concatenate(
        [jnp.full((n,), -1.0 if neg else 1.0, jnp.float32) for n, neg in zip(sizes, flips)]
    )[:, None, None]
    own = jnp.concatenate(blocks, axis=0) if len(blocks) > 1 else blocks[0]
    tops = own[:, -WIDE:, :]
    bots = own[:, :WIDE, :]
    south = lax.ppermute(tops, "oy", [(i, i + 1) for i in range(rows_n - 1)])
    north = lax.ppermute(bots, "oy", [(i + 1, i) for i in range(rows_n - 1)])
    top_row = (rows_n - 1) * cols_n
    fold = lax.ppermute(
        tops,
        ("oy", "ox"),
        [(top_row + (cols_n // 2 - j) % cols_n, top_row + j) for j in range(cols_n)],
    )
    north = jnp.where(on_top, fold[:, ::-1, ::-1] * sign, north)
    easts = jnp.concatenate([own[..., -WIDE:], north[..., -WIDE:], south[..., -WIDE:]], axis=1)
    wests = jnp.concatenate([own[..., :WIDE], north[..., :WIDE], south[..., :WIDE]], axis=1)
    from_w = lax.ppermute(easts, "ox", [(i, (i + 1) % cols_n) for i in range(cols_n)])
    from_e = lax.ppermute(wests, "ox", [((i + 1) % cols_n, i) for i in range(cols_n)])
    out = []
    at = 0
    for b, n in zip(blocks, sizes):
        rows = jnp.concatenate([b, north[at:at + n], south[at:at + n]], axis=1)
        gap = jnp.zeros(rows.shape[:-1] + (LANES - b.shape[-1] - 2 * WIDE,), b.dtype)
        out.append(jnp.concatenate([rows, from_e[at:at + n], gap, from_w[at:at + n]], axis=-1))
        at += n
    return out


def stencil_kernel(s_ref, u_ref, v_ref, m_ref, f_ref, o_ref, buf, cw, ce, cs, cn, cc, m8, mf):
    nt, nk, rows, lanes = s_ref.shape
    mask = m_ref[...]
    m8[...] = mask * 0.08
    for t in range(nt):
        mf[t] = mask * f_ref[t]

    def coef(k, carry):
        u = u_ref[k]
        v = v_ref[k]
        up = jnp.maximum(u, 0.0)
        um = jnp.minimum(u, 0.0)
        vp = jnp.maximum(v, 0.0)
        vm = jnp.minimum(v, 0.0)
        cw[k] = mask * (up + 0.08)
        ce[k] = mask * (0.08 - um)
        cs[k] = mask * (vp + 0.08)
        cn[k] = mask * (0.08 - vm)
        cc[k] = mask * ((um - up) + (vm - vp) - 0.48)
        return carry

    lax.fori_loop(0, nk, coef, 0)
    buf[0] = s_ref[...]

    def plane(src, dst, t, k, above, below, forced):
        s = buf[src, t, k]
        west = pltpu.roll(s, 1, 1)
        east = pltpu.roll(s, lanes - 1, 1)
        south = pltpu.roll(s, 1, 0)
        north = pltpu.roll(s, rows - 1, 0)
        if above is None:
            above = s
        if below is None:
            below = s
        tend = cw[k] * west + ce[k] * east + cs[k] * south + cn[k] * north + cc[k] * s
        tend = tend + m8[...] * (above + below)
        if forced:
            tend = tend + mf[t]
        buf[dst, t, k] = s + tend

    def step(i, carry):
        src = i % 2
        dst = 1 - src
        for t in range(nt):
            plane(src, dst, t, 0, None, buf[src, t, 1], True)

            def mid(k, c):
                plane(src, dst, t, k, buf[src, t, k - 1], buf[src, t, k + 1], False)
                return c

            lax.fori_loop(1, nk - 1, mid, 0)
            plane(src, dst, t, nk - 1, buf[src, t, nk - 2], None, False)
        return carry

    lax.fori_loop(0, STEPS, step, 0)
    o_ref[...] = buf[STEPS % 2, :, :, : o_ref.shape[2], : o_ref.shape[3]]


def evolve(state, u_x, v_x, m_x, f_x, out_rows, out_cols):
    nt, nk, rows, lanes = state.shape
    plane = (rows, lanes)
    return pl.pallas_call(
        stencil_kernel,
        out_shape=jax.ShapeDtypeStruct((nt, nk, out_rows, out_cols), jnp.float32),
        scratch_shapes=[
            pltpu.VMEM((2, nt, nk) + plane, jnp.float32),
            pltpu.VMEM((nk,) + plane, jnp.float32),
            pltpu.VMEM((nk,) + plane, jnp.float32),
            pltpu.VMEM((nk,) + plane, jnp.float32),
            pltpu.VMEM((nk,) + plane, jnp.float32),
            pltpu.VMEM((nk,) + plane, jnp.float32),
            pltpu.VMEM(plane, jnp.float32),
            pltpu.VMEM((nt,) + plane, jnp.float32),
        ],
        compiler_params=pltpu.CompilerParams(vmem_limit_bytes=60 * 1024 * 1024),
    )(state, u_x, v_x, m_x, f_x)


def remap(padded, remap_index, remap_weight):
    nf, arows, acols = padded.shape
    kk, orows, ocols = remap_index.shape
    base_r = jnp.arange(orows, dtype=jnp.int32) * (arows - 2 * H - 1) // (orows - 1) + H
    base_c = jnp.arange(ocols, dtype=jnp.int32) * (acols - 2 * H - 1) // (ocols - 1) + H
    offs = jnp.arange(2 * H + 1, dtype=jnp.int32) - H
    pick_r = (
        (base_r[None, :, None] + offs[:, None, None])
        == jnp.arange(arows, dtype=jnp.int32)[None, None, :]
    ).astype(jnp.float32).reshape(-1, arows)
    pick_c = (
        jnp.arange(acols, dtype=jnp.int32)[:, None, None]
        == (base_c[None, None, :] + offs[None, :, None])
    ).astype(jnp.float32).reshape(acols, -1)
    lifted = jnp.einsum("pa,fab->fpb", pick_r, padded, precision=HIGH)
    window = jnp.einsum("fpb,bq->fpq", lifted, pick_c, precision=HIGH)
    window = window.reshape(nf, 2 * H + 1, orows, 2 * H + 1, ocols)
    row_of = remap_index // acols - base_r[None, :, None] + H
    col_of = remap_index % acols - base_c[None, None, :] + H
    inside = (row_of >= 0) & (row_of <= 2 * H) & (col_of >= 0) & (col_of <= 2 * H)
    slot = jnp.where(inside, row_of * (2 * H + 1) + col_of, -1)
    slots = jnp.arange((2 * H + 1) ** 2, dtype=jnp.int32)
    wsum = jnp.sum(
        jnp.where(slot[:, None] == slots[None, :, None, None], remap_weight[:, None], 0.0),
        axis=0,
    ).reshape(2 * H + 1, 2 * H + 1, orows, ocols)
    fast = jnp.sum(window * wsum.transpose(0, 2, 1, 3)[None], axis=(1, 3))
    missed = jnp.logical_not(jnp.all(inside))

    def general():
        flat = padded.reshape(nf, -1)
        total = jnp.zeros((nf,) + remap_index.shape[1:], jnp.float32)
        for source in range(kk):
            picked = jnp.take(flat, remap_index[source], axis=1)
            total = total + remap_weight[source][None] * picked
        return total

    return lax.cond(missed, general, lambda: fast)


def on_device(atm_flux, remap_index, remap_weight, coupling, land_mask, tracers, u_vel, v_vel):
    lev = tracers.shape[1]
    fields = [
        tracers.reshape((-1,) + tracers.shape[2:]),
        u_vel.astype(jnp.float32),
        v_vel.astype(jnp.float32),
        land_mask.astype(jnp.float32)[None],
    ]
    state, u_x, v_x, m_x = extend(fields, [False, True, True, False])
    state = state.reshape((-1, lev) + state.shape[1:])

    atm_tile = lax.all_to_all(atm_flux, "ox", split_axis=2, concat_axis=1, tiled=True)
    lon_wide = with_halo(atm_tile, (("ox", 2),), H, True)
    padded = with_halo(lon_wide, (("oy", 1),), H, False)
    ocean_flux = remap(padded, remap_index, remap_weight)
    forcing = jnp.einsum("tf,frc->trc", coupling, ocean_flux, precision=HIGH)
    (f_x,) = extend([forcing], [False])
    rows, cols = tracers.shape[-2:]
    final = evolve(state, u_x, v_x, m_x[0], f_x, rows, cols)
    return (ocean_flux, final)


def solution(mesh):
    placed = (
        P(None, ("oy", "ox"), None),
        P(None, "oy", "ox"),
        P(None, "oy", "ox"),
        P(),
        P("oy", "ox"),
        P(None, None, "oy", "ox"),
        P(None, "oy", "ox"),
        P(None, "oy", "ox"),
    )
    return jax.shard_map(
        on_device,
        mesh=mesh,
        in_specs=placed,
        out_specs=(P(None, "oy", "ox"), P(None, None, "oy", "ox")),
        check_vma=False,
    )
```

```python
import jax
import jax.numpy as jnp
from jax import lax
from jax.sharding import PartitionSpec as P
from jax.experimental import pallas as pl
from jax.experimental.pallas import tpu as pltpu

H = 2
STEPS = 8
WIDE = 8
LANES = 384
HIGH = lax.Precision.HIGHEST


def with_halo(cells, sides, width, closed):
    for axis, dim in sides:
        count = lax.axis_size(axis)
        ends = count if closed else count - 1
        head = lax.slice_in_dim(cells, 0, width, axis=dim)
        tail = lax.slice_in_dim(cells, cells.shape[dim] - width, cells.shape[dim], axis=dim)
        cells = jnp.concatenate(
            [
                lax.ppermute(tail, axis, [(i, (i + 1) % count) for i in range(ends)]),
                cells,
                lax.ppermute(head, axis, [((i + 1) % count, i) for i in range(ends)]),
            ],
            axis=dim,
        )
    return cells


def extend(blocks, flips):
    rows_n = lax.axis_size("oy")
    cols_n = lax.axis_size("ox")
    on_top = lax.axis_index("oy") == rows_n - 1
    sizes = [b.shape[0] for b in blocks]
    sign = jnp.concatenate(
        [jnp.full((n,), -1.0 if neg else 1.0, jnp.float32) for n, neg in zip(sizes, flips)]
    )[:, None, None]
    own = jnp.concatenate(blocks, axis=0) if len(blocks) > 1 else blocks[0]
    tops = own[:, -WIDE:, :]
    bots = own[:, :WIDE, :]
    south = lax.ppermute(tops, "oy", [(i, i + 1) for i in range(rows_n - 1)])
    north = lax.ppermute(bots, "oy", [(i + 1, i) for i in range(rows_n - 1)])
    top_row = (rows_n - 1) * cols_n
    fold = lax.ppermute(
        tops,
        ("oy", "ox"),
        [(top_row + (cols_n // 2 - j) % cols_n, top_row + j) for j in range(cols_n)],
    )
    north = jnp.where(on_top, fold[:, ::-1, ::-1] * sign, north)
    easts = jnp.concatenate([own[..., -WIDE:], north[..., -WIDE:], south[..., -WIDE:]], axis=1)
    wests = jnp.concatenate([own[..., :WIDE], north[..., :WIDE], south[..., :WIDE]], axis=1)
    from_w = lax.ppermute(easts, "ox", [(i, (i + 1) % cols_n) for i in range(cols_n)])
    from_e = lax.ppermute(wests, "ox", [((i + 1) % cols_n, i) for i in range(cols_n)])
    out = []
    at = 0
    for b, n in zip(blocks, sizes):
        rows = jnp.concatenate([b, north[at:at + n], south[at:at + n]], axis=1)
        gap = jnp.zeros(rows.shape[:-1] + (LANES - b.shape[-1] - 2 * WIDE,), b.dtype)
        out.append(jnp.concatenate([rows, from_e[at:at + n], gap, from_w[at:at + n]], axis=-1))
        at += n
    return out


def stencil_kernel(s_ref, u_ref, v_ref, m_ref, f_ref, o_ref, buf, cw, ce, cs, cn, cc, m8, mf):
    nt, nk, rows, lanes = s_ref.shape
    mask = m_ref[...]
    m8[...] = mask * 0.08
    for t in range(nt):
        mf[t] = mask * f_ref[t]

    def coef(k, carry):
        u = u_ref[k]
        v = v_ref[k]
        up = jnp.maximum(u, 0.0)
        um = jnp.minimum(u, 0.0)
        vp = jnp.maximum(v, 0.0)
        vm = jnp.minimum(v, 0.0)
        cw[k] = mask * (up + 0.08)
        ce[k] = mask * (0.08 - um)
        cs[k] = mask * (vp + 0.08)
        cn[k] = mask * (0.08 - vm)
        cc[k] = mask * ((um - up) + (vm - vp) - 0.48)
        return carry

    lax.fori_loop(0, nk, coef, 0)
    buf[0] = s_ref[...]

    strips = rows // 8

    def plane(src, dst, k, above, below, forced):
        for i in range(strips):
            r0 = i * 8
            rp = (i - 1) % strips * 8
            rn = (i + 1) % strips * 8
            at = pl.ds(r0, 8)
            c_w = cw[k, at, :]
            c_e = ce[k, at, :]
            c_s = cs[k, at, :]
            c_n = cn[k, at, :]
            c_c = cc[k, at, :]
            c_8 = m8[at, :]
            for t in range(nt):
                cur = buf[src, t, k, at, :]
                prev = buf[src, t, k, pl.ds(rp, 8), :]
                nxt = buf[src, t, k, pl.ds(rn, 8), :]
                south = pltpu.roll(jnp.concatenate([prev, cur], axis=0), 1, 0)[8:]
                north = pltpu.roll(jnp.concatenate([cur, nxt], axis=0), 15, 0)[:8]
                west = pltpu.roll(cur, 1, 1)
                east = pltpu.roll(cur, lanes - 1, 1)
                up = cur if above is None else buf[src, t, above, at, :]
                down = cur if below is None else buf[src, t, below, at, :]
                tend = c_w * west + c_e * east + c_s * south + c_n * north + c_c * cur
                tend = tend + c_8 * (up + down)
                if forced:
                    tend = tend + mf[t, at, :]
                buf[dst, t, k, at, :] = cur + tend

    def step(i, carry):
        src = i % 2
        dst = 1 - src
        plane(src, dst, 0, None, 1, True)

        def mid(k, c):
            plane(src, dst, k, k - 1, k + 1, False)
            return c

        lax.fori_loop(1, nk - 1, mid, 0)
        plane(src, dst, nk - 1, nk - 2, None, False)
        return carry

    lax.fori_loop(0, STEPS, step, 0)
    o_ref[...] = buf[STEPS % 2, :, :, : o_ref.shape[2], : o_ref.shape[3]]


def evolve(state, u_x, v_x, m_x, f_x, out_rows, out_cols):
    nt, nk, rows, lanes = state.shape
    plane = (rows, lanes)
    return pl.pallas_call(
        stencil_kernel,
        out_shape=jax.ShapeDtypeStruct((nt, nk, out_rows, out_cols), jnp.float32),
        scratch_shapes=[
            pltpu.VMEM((2, nt, nk) + plane, jnp.float32),
            pltpu.VMEM((nk,) + plane, jnp.float32),
            pltpu.VMEM((nk,) + plane, jnp.float32),
            pltpu.VMEM((nk,) + plane, jnp.float32),
            pltpu.VMEM((nk,) + plane, jnp.float32),
            pltpu.VMEM((nk,) + plane, jnp.float32),
            pltpu.VMEM(plane, jnp.float32),
            pltpu.VMEM((nt,) + plane, jnp.float32),
        ],
        compiler_params=pltpu.CompilerParams(vmem_limit_bytes=60 * 1024 * 1024),
    )(state, u_x, v_x, m_x, f_x)


def remap(padded, remap_index, remap_weight):
    nf, arows, acols = padded.shape
    kk, orows, ocols = remap_index.shape
    base_r = jnp.arange(orows, dtype=jnp.int32) * (arows - 2 * H - 1) // (orows - 1) + H
    base_c = jnp.arange(ocols, dtype=jnp.int32) * (acols - 2 * H - 1) // (ocols - 1) + H
    offs = jnp.arange(2 * H + 1, dtype=jnp.int32) - H
    pick_r = (
        (base_r[None, :, None] + offs[:, None, None])
        == jnp.arange(arows, dtype=jnp.int32)[None, None, :]
    ).astype(jnp.float32).reshape(-1, arows)
    pick_c = (
        jnp.arange(acols, dtype=jnp.int32)[:, None, None]
        == (base_c[None, None, :] + offs[None, :, None])
    ).astype(jnp.float32).reshape(acols, -1)
    lifted = jnp.einsum("pa,fab->fpb", pick_r, padded, precision=HIGH)
    window = jnp.einsum("fpb,bq->fpq", lifted, pick_c, precision=HIGH)
    window = window.reshape(nf, 2 * H + 1, orows, 2 * H + 1, ocols)
    row_of = remap_index // acols - base_r[None, :, None] + H
    col_of = remap_index % acols - base_c[None, None, :] + H
    inside = (row_of >= 0) & (row_of <= 2 * H) & (col_of >= 0) & (col_of <= 2 * H)
    slot = jnp.where(inside, row_of * (2 * H + 1) + col_of, -1)
    slots = jnp.arange((2 * H + 1) ** 2, dtype=jnp.int32)
    wsum = jnp.sum(
        jnp.where(slot[:, None] == slots[None, :, None, None], remap_weight[:, None], 0.0),
        axis=0,
    ).reshape(2 * H + 1, 2 * H + 1, orows, ocols)
    fast = jnp.sum(window * wsum.transpose(0, 2, 1, 3)[None], axis=(1, 3))
    missed = jnp.logical_not(jnp.all(inside))

    def general():
        flat = padded.reshape(nf, -1)
        total = jnp.zeros((nf,) + remap_index.shape[1:], jnp.float32)
        for source in range(kk):
            picked = jnp.take(flat, remap_index[source], axis=1)
            total = total + remap_weight[source][None] * picked
        return total

    return lax.cond(missed, general, lambda: fast)


def on_device(atm_flux, remap_index, remap_weight, coupling, land_mask, tracers, u_vel, v_vel):
    lev = tracers.shape[1]
    fields = [
        tracers.reshape((-1,) + tracers.shape[2:]),
        u_vel.astype(jnp.float32),
        v_vel.astype(jnp.float32),
        land_mask.astype(jnp.float32)[None],
    ]
    state, u_x, v_x, m_x = extend(fields, [False, True, True, False])
    state = state.reshape((-1, lev) + state.shape[1:])

    atm_tile = lax.all_to_all(atm_flux, "ox", split_axis=2, concat_axis=1, tiled=True)
    lon_wide = with_halo(atm_tile, (("ox", 2),), H, True)
    padded = with_halo(lon_wide, (("oy", 1),), H, False)
    ocean_flux = remap(padded, remap_index, remap_weight)
    forcing = jnp.sum(coupling[:, :, None, None] * ocean_flux[None], axis=1)
    (f_x,) = extend([forcing], [False])
    rows, cols = tracers.shape[-2:]
    final = evolve(state, u_x, v_x, m_x[0], f_x, rows, cols)
    return (ocean_flux, final)


def solution(mesh):
    placed = (
        P(None, ("oy", "ox"), None),
        P(None, "oy", "ox"),
        P(None, "oy", "ox"),
        P(),
        P("oy", "ox"),
        P(None, None, "oy", "ox"),
        P(None, "oy", "ox"),
        P(None, "oy", "ox"),
    )
    return jax.shard_map(
        on_device,
        mesh=mesh,
        in_specs=placed,
        out_specs=(P(None, "oy", "ox"), P(None, None, "oy", "ox")),
        check_vma=False,
    )
```

```python
import jax
import jax.numpy as jnp
from jax import lax
from jax.sharding import PartitionSpec as P
from jax.experimental import pallas as pl
from jax.experimental.pallas import tpu as pltpu

H = 2
STEPS = 8
WIDE = 8
LANES = 384
HIGH = lax.Precision.HIGHEST


def with_halo(cells, sides, width, closed):
    for axis, dim in sides:
        count = lax.axis_size(axis)
        ends = count if closed else count - 1
        head = lax.slice_in_dim(cells, 0, width, axis=dim)
        tail = lax.slice_in_dim(cells, cells.shape[dim] - width, cells.shape[dim], axis=dim)
        cells = jnp.concatenate(
            [
                lax.ppermute(tail, axis, [(i, (i + 1) % count) for i in range(ends)]),
                cells,
                lax.ppermute(head, axis, [((i + 1) % count, i) for i in range(ends)]),
            ],
            axis=dim,
        )
    return cells


def exchange(blocks, flips):
    rows_n = lax.axis_size("oy")
    cols_n = lax.axis_size("ox")
    on_top = lax.axis_index("oy") == rows_n - 1
    sizes = [b.shape[0] for b in blocks]
    sign = jnp.concatenate(
        [jnp.full((n,), -1.0 if neg else 1.0, jnp.float32) for n, neg in zip(sizes, flips)]
    )[:, None, None]
    tops = jnp.concatenate([b[:, -WIDE:, :] for b in blocks], axis=0)
    bots = jnp.concatenate([b[:, :WIDE, :] for b in blocks], axis=0)
    south = lax.ppermute(tops, "oy", [(i, i + 1) for i in range(rows_n - 1)])
    north = lax.ppermute(bots, "oy", [(i + 1, i) for i in range(rows_n - 1)])
    top_row = (rows_n - 1) * cols_n
    fold = lax.ppermute(
        tops,
        ("oy", "ox"),
        [(top_row + (cols_n // 2 - j) % cols_n, top_row + j) for j in range(cols_n)],
    )
    north = jnp.where(on_top, fold[:, ::-1, ::-1] * sign, north)
    easts = jnp.concatenate(
        [jnp.concatenate([b[..., -WIDE:] for b in blocks], axis=0), north[..., -WIDE:], south[..., -WIDE:]],
        axis=1,
    )
    wests = jnp.concatenate(
        [jnp.concatenate([b[..., :WIDE] for b in blocks], axis=0), north[..., :WIDE], south[..., :WIDE]],
        axis=1,
    )
    from_w = lax.ppermute(easts, "ox", [(i, (i + 1) % cols_n) for i in range(cols_n)])
    from_e = lax.ppermute(wests, "ox", [((i + 1) % cols_n, i) for i in range(cols_n)])
    gap = jnp.zeros(from_e.shape[:-1] + (LANES - blocks[0].shape[-1] - 2 * WIDE,), jnp.float32)
    return north, south, jnp.concatenate([from_e, gap, from_w], axis=-1)


def stencil_kernel(tr_ref, u_ref, v_ref, m_ref, f_ref, hn_ref, hs_ref, hc_ref, fn_ref, fs_ref, fc_ref,
                   o_ref, buf, uu, vv, mm, ff, cw, ce, cs, cn, cc, m8, mf):
    nt, nk, orows, ocols = tr_ref.shape
    _, planes, rows, lanes = buf.shape

    def place(dst, own, at):
        dst[:orows, :ocols] = own
        dst[orows:orows + WIDE, :ocols] = hn_ref[at]
        dst[orows + WIDE:, :ocols] = hs_ref[at]
        dst[:, ocols:] = hc_ref[at]

    def fill(p, carry):
        place(buf.at[0, p], tr_ref[p // nk, p % nk], p)
        return carry

    lax.fori_loop(0, planes, fill, 0)

    def fill_uv(k, carry):
        place(uu.at[k], u_ref[k].astype(jnp.float32), planes + k)
        place(vv.at[k], v_ref[k].astype(jnp.float32), planes + nk + k)
        return carry

    lax.fori_loop(0, nk, fill_uv, 0)
    place(mm, m_ref[...].astype(jnp.float32), planes + 2 * nk)
    for t in range(nt):
        ff[t, :orows, :ocols] = f_ref[t]
        ff[t, orows:orows + WIDE, :ocols] = fn_ref[t]
        ff[t, orows + WIDE:, :ocols] = fs_ref[t]
        ff[t, :, ocols:] = fc_ref[t]

    mask = mm[...]
    m8[...] = mask * 0.08
    for t in range(nt):
        mf[t] = mask * ff[t]

    def coef(k, carry):
        u = uu[k]
        v = vv[k]
        up = jnp.maximum(u, 0.0)
        um = jnp.minimum(u, 0.0)
        vp = jnp.maximum(v, 0.0)
        vm = jnp.minimum(v, 0.0)
        cw[k] = mask * (up + 0.08)
        ce[k] = mask * (0.08 - um)
        cs[k] = mask * (vp + 0.08)
        cn[k] = mask * (0.08 - vm)
        cc[k] = mask * ((um - up) + (vm - vp) - 0.48)
        return carry

    lax.fori_loop(0, nk, coef, 0)

    def plane(src, dst, t, k, above, below, forced):
        p = t * nk + k
        s = buf[src, p]
        west = pltpu.roll(s, 1, 1)
        east = pltpu.roll(s, lanes - 1, 1)
        south = pltpu.roll(s, 1, 0)
        north = pltpu.roll(s, rows - 1, 0)
        above = s if above is None else buf[src, t * nk + above]
        below = s if below is None else buf[src, t * nk + below]
        tend = cw[k] * west + ce[k] * east + cs[k] * south + cn[k] * north + cc[k] * s
        tend = tend + m8[...] * (above + below)
        if forced:
            tend = tend + mf[t]
        buf[dst, p] = s + tend

    def step(i, carry):
        src = i % 2
        dst = 1 - src
        for t in range(nt):
            plane(src, dst, t, 0, None, 1, True)

            def mid(k, c):
                plane(src, dst, t, k, k - 1, k + 1, False)
                return c

            lax.fori_loop(1, nk - 1, mid, 0)
            plane(src, dst, t, nk - 1, nk - 2, None, False)
        return carry

    lax.fori_loop(0, STEPS, step, 0)

    def out(p, carry):
        o_ref[p // nk, p % nk] = buf[STEPS % 2, p, :orows, :ocols]
        return carry

    lax.fori_loop(0, planes, out, 0)


def evolve(tracers, u_vel, v_vel, land_mask, forcing, halo, f_halo):
    nt, nk, orows, ocols = tracers.shape
    plane = (orows + 2 * WIDE, LANES)
    vm = lambda *shape: pltpu.VMEM(shape, jnp.float32)
    return pl.pallas_call(
        stencil_kernel,
        out_shape=jax.ShapeDtypeStruct(tracers.shape, jnp.float32),
        scratch_shapes=[
            vm(2, nt * nk, *plane),
            vm(nk, *plane),
            vm(nk, *plane),
            vm(*plane),
            vm(nt, *plane),
            vm(nk, *plane),
            vm(nk, *plane),
            vm(nk, *plane),
            vm(nk, *plane),
            vm(nk, *plane),
            vm(*plane),
            vm(nt, *plane),
        ],
        compiler_params=pltpu.CompilerParams(vmem_limit_bytes=62 * 1024 * 1024),
    )(tracers, u_vel, v_vel, land_mask, forcing, *halo, *f_halo)


def remap(padded, remap_index, remap_weight):
    nf, arows, acols = padded.shape
    kk, orows, ocols = remap_index.shape
    base_r = jnp.arange(orows, dtype=jnp.int32) * (arows - 2 * H - 1) // (orows - 1) + H
    base_c = jnp.arange(ocols, dtype=jnp.int32) * (acols - 2 * H - 1) // (ocols - 1) + H
    offs = jnp.arange(2 * H + 1, dtype=jnp.int32) - H
    pick_r = (
        (base_r[None, :, None] + offs[:, None, None])
        == jnp.arange(arows, dtype=jnp.int32)[None, None, :]
    ).astype(jnp.float32).reshape(-1, arows)
    pick_c = (
        jnp.arange(acols, dtype=jnp.int32)[:, None, None]
        == (base_c[None, None, :] + offs[None, :, None])
    ).astype(jnp.float32).reshape(acols, -1)
    lifted = jnp.einsum("pa,fab->fpb", pick_r, padded, precision=HIGH)
    window = jnp.einsum("fpb,bq->fpq", lifted, pick_c, precision=HIGH)
    window = window.reshape(nf, 2 * H + 1, orows, 2 * H + 1, ocols)
    row_of = remap_index // acols - base_r[None, :, None] + H
    col_of = remap_index % acols - base_c[None, None, :] + H
    inside = (row_of >= 0) & (row_of <= 2 * H) & (col_of >= 0) & (col_of <= 2 * H)
    slot = jnp.where(inside, row_of * (2 * H + 1) + col_of, -1)
    slots = jnp.arange((2 * H + 1) ** 2, dtype=jnp.int32)
    wsum = jnp.sum(
        jnp.where(slot[:, None] == slots[None, :, None, None], remap_weight[:, None], 0.0),
        axis=0,
    ).reshape(2 * H + 1, 2 * H + 1, orows, ocols)
    fast = jnp.sum(window * wsum.transpose(0, 2, 1, 3)[None], axis=(1, 3))
    missed = jnp.logical_not(jnp.all(inside))

    def general():
        flat = padded.reshape(nf, -1)
        total = jnp.zeros((nf,) + remap_index.shape[1:], jnp.float32)
        for source in range(kk):
            picked = jnp.take(flat, remap_index[source], axis=1)
            total = total + remap_weight[source][None] * picked
        return total

    return lax.cond(missed, general, lambda: fast)


def on_device(atm_flux, remap_index, remap_weight, coupling, land_mask, tracers, u_vel, v_vel):
    fields = [
        tracers.reshape((-1,) + tracers.shape[2:]),
        u_vel.astype(jnp.float32),
        v_vel.astype(jnp.float32),
        land_mask.astype(jnp.float32)[None],
    ]
    halo = exchange(fields, [False, True, True, False])

    atm_tile = lax.all_to_all(atm_flux, "ox", split_axis=2, concat_axis=1, tiled=True)
    lon_wide = with_halo(atm_tile, (("ox", 2),), H, True)
    padded = with_halo(lon_wide, (("oy", 1),), H, False)
    ocean_flux = remap(padded, remap_index, remap_weight)
    forcing = jnp.sum(coupling[:, :, None, None] * ocean_flux[None], axis=1)
    f_halo = exchange([forcing], [False])
    final = evolve(tracers, u_vel, v_vel, land_mask, forcing, halo, f_halo)
    return (ocean_flux, final)


def solution(mesh):
    placed = (
        P(None, ("oy", "ox"), None),
        P(None, "oy", "ox"),
        P(None, "oy", "ox"),
        P(),
        P("oy", "ox"),
        P(None, None, "oy", "ox"),
        P(None, "oy", "ox"),
        P(None, "oy", "ox"),
    )
    return jax.shard_map(
        on_device,
        mesh=mesh,
        in_specs=placed,
        out_specs=(P(None, "oy", "ox"), P(None, None, "oy", "ox")),
        check_vma=False,
    )
```

```python
import jax
import jax.numpy as jnp
from jax import lax
from jax.sharding import PartitionSpec as P
from jax.experimental import pallas as pl
from jax.experimental.pallas import tpu as pltpu

H = 2
STEPS = 8
WIDE = 8
LANES = 384
HIGH = lax.Precision.HIGHEST


def with_halo(cells, sides, width, closed):
    for axis, dim in sides:
        count = lax.axis_size(axis)
        ends = count if closed else count - 1
        head = lax.slice_in_dim(cells, 0, width, axis=dim)
        tail = lax.slice_in_dim(cells, cells.shape[dim] - width, cells.shape[dim], axis=dim)
        cells = jnp.concatenate(
            [
                lax.ppermute(tail, axis, [(i, (i + 1) % count) for i in range(ends)]),
                cells,
                lax.ppermute(head, axis, [((i + 1) % count, i) for i in range(ends)]),
            ],
            axis=dim,
        )
    return cells


def exchange(blocks, flips):
    rows_n = lax.axis_size("oy")
    cols_n = lax.axis_size("ox")
    on_top = lax.axis_index("oy") == rows_n - 1
    sizes = [b.shape[0] for b in blocks]
    sign = jnp.concatenate(
        [jnp.full((n,), -1.0 if neg else 1.0, jnp.float32) for n, neg in zip(sizes, flips)]
    )[:, None, None]
    tops = jnp.concatenate([b[:, -WIDE:, :] for b in blocks], axis=0)
    bots = jnp.concatenate([b[:, :WIDE, :] for b in blocks], axis=0)
    south = lax.ppermute(tops, "oy", [(i, i + 1) for i in range(rows_n - 1)])
    north = lax.ppermute(bots, "oy", [(i + 1, i) for i in range(rows_n - 1)])
    top_row = (rows_n - 1) * cols_n
    fold = lax.ppermute(
        tops,
        ("oy", "ox"),
        [(top_row + (cols_n // 2 - j) % cols_n, top_row + j) for j in range(cols_n)],
    )
    north = jnp.where(on_top, fold[:, ::-1, ::-1] * sign, north)
    easts = jnp.concatenate(
        [jnp.concatenate([b[..., -WIDE:] for b in blocks], axis=0), north[..., -WIDE:], south[..., -WIDE:]],
        axis=1,
    )
    wests = jnp.concatenate(
        [jnp.concatenate([b[..., :WIDE] for b in blocks], axis=0), north[..., :WIDE], south[..., :WIDE]],
        axis=1,
    )
    from_w = lax.ppermute(easts, "ox", [(i, (i + 1) % cols_n) for i in range(cols_n)])
    from_e = lax.ppermute(wests, "ox", [((i + 1) % cols_n, i) for i in range(cols_n)])
    gap = jnp.zeros(from_e.shape[:-1] + (LANES - blocks[0].shape[-1] - 2 * WIDE,), jnp.float32)
    return north, south, jnp.concatenate([from_e, gap, from_w], axis=-1)


def stencil_kernel(tr_ref, u_ref, v_ref, m_ref, f_ref, hn_ref, hs_ref, hc_ref, fn_ref, fs_ref, fc_ref,
                   o_ref, buf, uu, vv, mm, ff, cw, ce, cs, cn, cc, m8, mf):
    nt, nk, orows, ocols = tr_ref.shape
    _, planes, rows, lanes = buf.shape

    def place(dst, own, at):
        dst[:orows, :ocols] = own
        dst[orows:orows + WIDE, :ocols] = hn_ref[at]
        dst[orows + WIDE:, :ocols] = hs_ref[at]
        dst[:, ocols:] = hc_ref[at]

    def fill(p, carry):
        place(buf.at[0, p], tr_ref[p // nk, p % nk], p)
        return carry

    lax.fori_loop(0, planes, fill, 0)

    def fill_uv(k, carry):
        place(uu.at[k], u_ref[k].astype(jnp.float32), planes + k)
        place(vv.at[k], v_ref[k].astype(jnp.float32), planes + nk + k)
        return carry

    lax.fori_loop(0, nk, fill_uv, 0)
    place(mm, m_ref[...].astype(jnp.float32), planes + 2 * nk)
    for t in range(nt):
        ff[t, :orows, :ocols] = f_ref[t]
        ff[t, orows:orows + WIDE, :ocols] = fn_ref[t]
        ff[t, orows + WIDE:, :ocols] = fs_ref[t]
        ff[t, :, ocols:] = fc_ref[t]

    mask = mm[...]
    m8[...] = mask * 0.08
    for t in range(nt):
        mf[t] = mask * ff[t]

    def coef(k, carry):
        u = uu[k]
        v = vv[k]
        up = jnp.maximum(u, 0.0)
        um = jnp.minimum(u, 0.0)
        vp = jnp.maximum(v, 0.0)
        vm = jnp.minimum(v, 0.0)
        cw[k] = mask * (up + 0.08)
        ce[k] = mask * (0.08 - um)
        cs[k] = mask * (vp + 0.08)
        cn[k] = mask * (0.08 - vm)
        cc[k] = mask * ((um - up) + (vm - vp) - 0.48)
        return carry

    lax.fori_loop(0, nk, coef, 0)

    def plane(src, dst, t, k, above, below, forced):
        p = t * nk + k
        s = buf[src, p]
        west = pltpu.roll(s, 1, 1)
        east = pltpu.roll(s, lanes - 1, 1)
        south = pltpu.roll(s, 1, 0)
        north = pltpu.roll(s, rows - 1, 0)
        above = s if above is None else buf[src, t * nk + above]
        below = s if below is None else buf[src, t * nk + below]
        tend = cw[k] * west + ce[k] * east + cs[k] * south + cn[k] * north + cc[k] * s
        tend = tend + m8[...] * (above + below)
        if forced:
            tend = tend + mf[t]
        buf[dst, p] = s + tend

    def step(i, carry):
        src = i % 2
        dst = 1 - src
        for t in range(nt):
            plane(src, dst, t, 0, None, 1, True)

            def mid(k, c):
                plane(src, dst, t, k, k - 1, k + 1, False)
                return c

            lax.fori_loop(1, nk - 1, mid, 0)
            plane(src, dst, t, nk - 1, nk - 2, None, False)
        return carry

    lax.fori_loop(0, STEPS, step, 0)

    def out(p, carry):
        o_ref[p // nk, p % nk] = buf[STEPS % 2, p, :orows, :ocols]
        return carry

    lax.fori_loop(0, planes, out, 0)


def evolve(tracers, u_vel, v_vel, land_mask, forcing, halo, f_halo):
    nt, nk, orows, ocols = tracers.shape
    plane = (orows + 2 * WIDE, LANES)
    vm = lambda *shape: pltpu.VMEM(shape, jnp.float32)
    return pl.pallas_call(
        stencil_kernel,
        out_shape=jax.ShapeDtypeStruct(tracers.shape, jnp.float32),
        scratch_shapes=[
            vm(2, nt * nk, *plane),
            vm(nk, *plane),
            vm(nk, *plane),
            vm(*plane),
            vm(nt, *plane),
            vm(nk, *plane),
            vm(nk, *plane),
            vm(nk, *plane),
            vm(nk, *plane),
            vm(nk, *plane),
            vm(*plane),
            vm(nt, *plane),
        ],
        compiler_params=pltpu.CompilerParams(vmem_limit_bytes=62 * 1024 * 1024),
    )(tracers, u_vel, v_vel, land_mask, forcing, *halo, *f_halo)


def atmosphere_block(atm_flux):
    cols_n = lax.axis_size("ox")
    rows_n = lax.axis_size("oy")
    band = lax.all_gather(atm_flux, "ox", axis=1, tiled=True)
    width = band.shape[2] // cols_n
    ring = jnp.concatenate([band[..., -H:], band, band[..., :H]], axis=2)
    own = lax.dynamic_slice_in_dim(ring, lax.axis_index("ox") * width, width + 2 * H, axis=2)
    below = lax.ppermute(own[:, -H:], "oy", [(i, i + 1) for i in range(rows_n - 1)])
    above = lax.ppermute(own[:, :H], "oy", [(i + 1, i) for i in range(rows_n - 1)])
    return jnp.concatenate([below, own, above], axis=1)


def remap(padded, remap_index, remap_weight):
    nf, arows, acols = padded.shape
    kk, orows, ocols = remap_index.shape
    base_r = jnp.arange(orows, dtype=jnp.int32) * (arows - 2 * H - 1) // (orows - 1) + H
    base_c = jnp.arange(ocols, dtype=jnp.int32) * (acols - 2 * H - 1) // (ocols - 1) + H
    offs = jnp.arange(2 * H + 1, dtype=jnp.int32) - H
    pick_r = (
        (base_r[None, :, None] + offs[:, None, None])
        == jnp.arange(arows, dtype=jnp.int32)[None, None, :]
    ).astype(jnp.float32).reshape(-1, arows)
    pick_c = (
        jnp.arange(acols, dtype=jnp.int32)[:, None, None]
        == (base_c[None, None, :] + offs[None, :, None])
    ).astype(jnp.float32).reshape(acols, -1)
    lifted = jnp.einsum("pa,fab->fpb", pick_r, padded, precision=HIGH)
    window = jnp.einsum("fpb,bq->fpq", lifted, pick_c, precision=HIGH)
    window = window.reshape(nf, 2 * H + 1, orows, 2 * H + 1, ocols)
    row_of = remap_index // acols - base_r[None, :, None] + H
    col_of = remap_index % acols - base_c[None, None, :] + H
    inside = (row_of >= 0) & (row_of <= 2 * H) & (col_of >= 0) & (col_of <= 2 * H)
    slot = jnp.where(inside, row_of * (2 * H + 1) + col_of, -1)
    slots = jnp.arange((2 * H + 1) ** 2, dtype=jnp.int32)
    wsum = jnp.sum(
        jnp.where(slot[:, None] == slots[None, :, None, None], remap_weight[:, None], 0.0),
        axis=0,
    ).reshape(2 * H + 1, 2 * H + 1, orows, ocols)
    fast = jnp.sum(window * wsum.transpose(0, 2, 1, 3)[None], axis=(1, 3))
    missed = jnp.logical_not(jnp.all(inside))

    def general():
        flat = padded.reshape(nf, -1)
        total = jnp.zeros((nf,) + remap_index.shape[1:], jnp.float32)
        for source in range(kk):
            picked = jnp.take(flat, remap_index[source], axis=1)
            total = total + remap_weight[source][None] * picked
        return total

    return lax.cond(missed, general, lambda: fast)


def on_device(atm_flux, remap_index, remap_weight, coupling, land_mask, tracers, u_vel, v_vel):
    fields = [
        tracers.reshape((-1,) + tracers.shape[2:]),
        u_vel.astype(jnp.float32),
        v_vel.astype(jnp.float32),
        land_mask.astype(jnp.float32)[None],
    ]
    halo = exchange(fields, [False, True, True, False])

    padded = atmosphere_block(atm_flux)
    ocean_flux = remap(padded, remap_index, remap_weight)
    forcing = jnp.sum(coupling[:, :, None, None] * ocean_flux[None], axis=1)
    f_halo = exchange([forcing], [False])
    final = evolve(tracers, u_vel, v_vel, land_mask, forcing, halo, f_halo)
    return (ocean_flux, final)


def solution(mesh):
    placed = (
        P(None, ("oy", "ox"), None),
        P(None, "oy", "ox"),
        P(None, "oy", "ox"),
        P(),
        P("oy", "ox"),
        P(None, None, "oy", "ox"),
        P(None, "oy", "ox"),
        P(None, "oy", "ox"),
    )
    return jax.shard_map(
        on_device,
        mesh=mesh,
        in_specs=placed,
        out_specs=(P(None, "oy", "ox"), P(None, None, "oy", "ox")),
        check_vma=False,
    )
```

```python
import jax
import jax.numpy as jnp
from jax import lax
from jax.sharding import PartitionSpec as P
from jax.experimental import pallas as pl
from jax.experimental.pallas import tpu as pltpu

H = 2
STEPS = 8
WIDE = 8
LANES = 384
HIGH = lax.Precision.HIGHEST


def with_halo(cells, sides, width, closed):
    for axis, dim in sides:
        count = lax.axis_size(axis)
        ends = count if closed else count - 1
        head = lax.slice_in_dim(cells, 0, width, axis=dim)
        tail = lax.slice_in_dim(cells, cells.shape[dim] - width, cells.shape[dim], axis=dim)
        cells = jnp.concatenate(
            [
                lax.ppermute(tail, axis, [(i, (i + 1) % count) for i in range(ends)]),
                cells,
                lax.ppermute(head, axis, [((i + 1) % count, i) for i in range(ends)]),
            ],
            axis=dim,
        )
    return cells


def exchange(blocks, flips):
    rows_n = lax.axis_size("oy")
    cols_n = lax.axis_size("ox")
    on_top = lax.axis_index("oy") == rows_n - 1
    sizes = [b.shape[0] for b in blocks]
    sign = jnp.concatenate(
        [jnp.full((n,), -1.0 if neg else 1.0, jnp.float32) for n, neg in zip(sizes, flips)]
    )[:, None, None]
    tops = jnp.concatenate([b[:, -WIDE:, :] for b in blocks], axis=0)
    bots = jnp.concatenate([b[:, :WIDE, :] for b in blocks], axis=0)
    south = lax.ppermute(tops, "oy", [(i, i + 1) for i in range(rows_n - 1)])
    north = lax.ppermute(bots, "oy", [(i + 1, i) for i in range(rows_n - 1)])
    top_row = (rows_n - 1) * cols_n
    fold = lax.ppermute(
        tops,
        ("oy", "ox"),
        [(top_row + (cols_n // 2 - j) % cols_n, top_row + j) for j in range(cols_n)],
    )
    north = jnp.where(on_top, fold[:, ::-1, ::-1] * sign, north)
    easts = jnp.concatenate(
        [jnp.concatenate([b[..., -WIDE:] for b in blocks], axis=0), north[..., -WIDE:], south[..., -WIDE:]],
        axis=1,
    )
    wests = jnp.concatenate(
        [jnp.concatenate([b[..., :WIDE] for b in blocks], axis=0), north[..., :WIDE], south[..., :WIDE]],
        axis=1,
    )
    from_w = lax.ppermute(easts, "ox", [(i, (i + 1) % cols_n) for i in range(cols_n)])
    from_e = lax.ppermute(wests, "ox", [((i + 1) % cols_n, i) for i in range(cols_n)])
    gap = jnp.zeros(from_e.shape[:-1] + (LANES - blocks[0].shape[-1] - 2 * WIDE,), jnp.float32)
    return north, south, jnp.concatenate([from_e, gap, from_w], axis=-1)


def stencil_kernel(tr_ref, u_ref, v_ref, m_ref, f_ref, hn_ref, hs_ref, hc_ref, fn_ref, fs_ref, fc_ref,
                   o_ref, buf, uu, vv, mm, ff, cw, ce, cs, cn, cc, m8, mf):
    nt, nk, orows, ocols = tr_ref.shape
    _, planes, rows, lanes = buf.shape

    def place(dst, own, at):
        dst[:orows, :ocols] = own
        dst[orows:orows + WIDE, :ocols] = hn_ref[at]
        dst[orows + WIDE:, :ocols] = hs_ref[at]
        dst[:, ocols:] = hc_ref[at]

    def fill(p, carry):
        place(buf.at[0, p], tr_ref[p // nk, p % nk], p)
        return carry

    lax.fori_loop(0, planes, fill, 0)

    def fill_uv(k, carry):
        place(uu.at[k], u_ref[k].astype(jnp.float32), planes + k)
        place(vv.at[k], v_ref[k].astype(jnp.float32), planes + nk + k)
        return carry

    lax.fori_loop(0, nk, fill_uv, 0)
    place(mm, m_ref[...].astype(jnp.float32), planes + 2 * nk)
    for t in range(nt):
        ff[t, :orows, :ocols] = f_ref[t]
        ff[t, orows:orows + WIDE, :ocols] = fn_ref[t]
        ff[t, orows + WIDE:, :ocols] = fs_ref[t]
        ff[t, :, ocols:] = fc_ref[t]

    mask = mm[...]
    m8[...] = mask * 0.08
    for t in range(nt):
        mf[t] = mask * ff[t]

    def coef(k, carry):
        u = uu[k]
        v = vv[k]
        up = jnp.maximum(u, 0.0)
        um = jnp.minimum(u, 0.0)
        vp = jnp.maximum(v, 0.0)
        vm = jnp.minimum(v, 0.0)
        cw[k] = mask * (up + 0.08)
        ce[k] = mask * (0.08 - um)
        cs[k] = mask * (vp + 0.08)
        cn[k] = mask * (0.08 - vm)
        cc[k] = mask * ((um - up) + (vm - vp) - 0.48)
        return carry

    lax.fori_loop(0, nk, coef, 0)

    def plane(src, dst, t, k, above, below, forced):
        p = t * nk + k
        s = buf[src, p]
        west = pltpu.roll(s, 1, 1)
        east = pltpu.roll(s, lanes - 1, 1)
        south = pltpu.roll(s, 1, 0)
        north = pltpu.roll(s, rows - 1, 0)
        above = s if above is None else buf[src, t * nk + above]
        below = s if below is None else buf[src, t * nk + below]
        tend = cw[k] * west + ce[k] * east + cs[k] * south + cn[k] * north + cc[k] * s
        tend = tend + m8[...] * (above + below)
        if forced:
            tend = tend + mf[t]
        buf[dst, p] = s + tend

    def step(i, carry):
        src = i % 2
        dst = 1 - src
        for t in range(nt):
            plane(src, dst, t, 0, None, 1, True)

            def mid(k, c):
                plane(src, dst, t, k, k - 1, k + 1, False)
                return c

            lax.fori_loop(1, nk - 1, mid, 0)
            plane(src, dst, t, nk - 1, nk - 2, None, False)
        return carry

    lax.fori_loop(0, STEPS, step, 0)

    def out(p, carry):
        o_ref[p // nk, p % nk] = buf[STEPS % 2, p, :orows, :ocols]
        return carry

    lax.fori_loop(0, planes, out, 0)


def evolve(tracers, u_vel, v_vel, land_mask, forcing, halo, f_halo):
    nt, nk, orows, ocols = tracers.shape
    plane = (orows + 2 * WIDE, LANES)
    vm = lambda *shape: pltpu.VMEM(shape, jnp.float32)
    return pl.pallas_call(
        stencil_kernel,
        out_shape=jax.ShapeDtypeStruct(tracers.shape, jnp.float32),
        scratch_shapes=[
            vm(2, nt * nk, *plane),
            vm(nk, *plane),
            vm(nk, *plane),
            vm(*plane),
            vm(nt, *plane),
            vm(nk, *plane),
            vm(nk, *plane),
            vm(nk, *plane),
            vm(nk, *plane),
            vm(nk, *plane),
            vm(*plane),
            vm(nt, *plane),
        ],
        compiler_params=pltpu.CompilerParams(vmem_limit_bytes=62 * 1024 * 1024),
    )(tracers, u_vel, v_vel, land_mask, forcing, *halo, *f_halo)


def atmosphere_block(atm_flux):
    cols_n = lax.axis_size("ox")
    rows_n = lax.axis_size("oy")
    width = atm_flux.shape[2] // cols_n
    ring = jnp.concatenate([atm_flux[..., -H:], atm_flux, atm_flux[..., :H]], axis=2)
    pieces = jnp.stack([ring[..., i * width:(i + 1) * width + 2 * H] for i in range(cols_n)])
    got = lax.all_to_all(pieces, "ox", split_axis=0, concat_axis=0, tiled=True)
    own = jnp.concatenate(list(got), axis=1)
    below = lax.ppermute(own[:, -H:], "oy", [(i, i + 1) for i in range(rows_n - 1)])
    above = lax.ppermute(own[:, :H], "oy", [(i + 1, i) for i in range(rows_n - 1)])
    return jnp.concatenate([below, own, above], axis=1)


def remap(padded, remap_index, remap_weight):
    nf, arows, acols = padded.shape
    kk, orows, ocols = remap_index.shape
    base_r = jnp.arange(orows, dtype=jnp.int32) * (arows - 2 * H - 1) // (orows - 1) + H
    base_c = jnp.arange(ocols, dtype=jnp.int32) * (acols - 2 * H - 1) // (ocols - 1) + H
    offs = jnp.arange(2 * H + 1, dtype=jnp.int32) - H
    pick_r = (
        (base_r[None, :, None] + offs[:, None, None])
        == jnp.arange(arows, dtype=jnp.int32)[None, None, :]
    ).astype(jnp.float32).reshape(-1, arows)
    pick_c = (
        jnp.arange(acols, dtype=jnp.int32)[:, None, None]
        == (base_c[None, None, :] + offs[None, :, None])
    ).astype(jnp.float32).reshape(acols, -1)
    lifted = jnp.einsum("pa,fab->fpb", pick_r, padded, precision=HIGH)
    window = jnp.einsum("fpb,bq->fpq", lifted, pick_c, precision=HIGH)
    window = window.reshape(nf, 2 * H + 1, orows, 2 * H + 1, ocols)
    row_of = remap_index // acols - base_r[None, :, None] + H
    col_of = remap_index % acols - base_c[None, None, :] + H
    inside = (row_of >= 0) & (row_of <= 2 * H) & (col_of >= 0) & (col_of <= 2 * H)
    slot = jnp.where(inside, row_of * (2 * H + 1) + col_of, -1)
    slots = jnp.arange((2 * H + 1) ** 2, dtype=jnp.int32)
    wsum = jnp.sum(
        jnp.where(slot[:, None] == slots[None, :, None, None], remap_weight[:, None], 0.0),
        axis=0,
    ).reshape(2 * H + 1, 2 * H + 1, orows, ocols)
    fast = jnp.sum(window * wsum.transpose(0, 2, 1, 3)[None], axis=(1, 3))
    missed = jnp.logical_not(jnp.all(inside))

    def general():
        flat = padded.reshape(nf, -1)
        total = jnp.zeros((nf,) + remap_index.shape[1:], jnp.float32)
        for source in range(kk):
            picked = jnp.take(flat, remap_index[source], axis=1)
            total = total + remap_weight[source][None] * picked
        return total

    return lax.cond(missed, general, lambda: fast)


def on_device(atm_flux, remap_index, remap_weight, coupling, land_mask, tracers, u_vel, v_vel):
    fields = [
        tracers.reshape((-1,) + tracers.shape[2:]),
        u_vel.astype(jnp.float32),
        v_vel.astype(jnp.float32),
        land_mask.astype(jnp.float32)[None],
    ]
    halo = exchange(fields, [False, True, True, False])

    padded = atmosphere_block(atm_flux)
    ocean_flux = remap(padded, remap_index, remap_weight)
    forcing = jnp.sum(coupling[:, :, None, None] * ocean_flux[None], axis=1)
    f_halo = exchange([forcing], [False])
    final = evolve(tracers, u_vel, v_vel, land_mask, forcing, halo, f_halo)
    return (ocean_flux, final)


def solution(mesh):
    placed = (
        P(None, ("oy", "ox"), None),
        P(None, "oy", "ox"),
        P(None, "oy", "ox"),
        P(),
        P("oy", "ox"),
        P(None, None, "oy", "ox"),
        P(None, "oy", "ox"),
        P(None, "oy", "ox"),
    )
    return jax.shard_map(
        on_device,
        mesh=mesh,
        in_specs=placed,
        out_specs=(P(None, "oy", "ox"), P(None, None, "oy", "ox")),
        check_vma=False,
    )
```

```python
import jax
import jax.numpy as jnp
from jax import lax
from jax.sharding import PartitionSpec as P
from jax.experimental import pallas as pl
from jax.experimental.pallas import tpu as pltpu

H = 2
STEPS = 8
WIDE = 8
LANES = 384
HIGH = lax.Precision.HIGHEST


def with_halo(cells, sides, width, closed):
    for axis, dim in sides:
        count = lax.axis_size(axis)
        ends = count if closed else count - 1
        head = lax.slice_in_dim(cells, 0, width, axis=dim)
        tail = lax.slice_in_dim(cells, cells.shape[dim] - width, cells.shape[dim], axis=dim)
        cells = jnp.concatenate(
            [
                lax.ppermute(tail, axis, [(i, (i + 1) % count) for i in range(ends)]),
                cells,
                lax.ppermute(head, axis, [((i + 1) % count, i) for i in range(ends)]),
            ],
            axis=dim,
        )
    return cells


def exchange(blocks, flips):
    rows_n = lax.axis_size("oy")
    cols_n = lax.axis_size("ox")
    on_top = lax.axis_index("oy") == rows_n - 1
    sizes = [b.shape[0] for b in blocks]
    sign = jnp.concatenate(
        [jnp.full((n,), -1.0 if neg else 1.0, jnp.float32) for n, neg in zip(sizes, flips)]
    )[:, None, None]
    tops = jnp.concatenate([b[:, -WIDE:, :] for b in blocks], axis=0)
    bots = jnp.concatenate([b[:, :WIDE, :] for b in blocks], axis=0)
    south = lax.ppermute(tops, "oy", [(i, i + 1) for i in range(rows_n - 1)])
    north = lax.ppermute(bots, "oy", [(i + 1, i) for i in range(rows_n - 1)])
    top_row = (rows_n - 1) * cols_n
    fold = lax.ppermute(
        tops,
        ("oy", "ox"),
        [(top_row + (cols_n // 2 - j) % cols_n, top_row + j) for j in range(cols_n)],
    )
    north = jnp.where(on_top, fold[:, ::-1, ::-1] * sign, north)
    easts = jnp.concatenate(
        [jnp.concatenate([b[..., -WIDE:] for b in blocks], axis=0), north[..., -WIDE:], south[..., -WIDE:]],
        axis=1,
    )
    wests = jnp.concatenate(
        [jnp.concatenate([b[..., :WIDE] for b in blocks], axis=0), north[..., :WIDE], south[..., :WIDE]],
        axis=1,
    )
    from_w = lax.ppermute(easts, "ox", [(i, (i + 1) % cols_n) for i in range(cols_n)])
    from_e = lax.ppermute(wests, "ox", [((i + 1) % cols_n, i) for i in range(cols_n)])
    gap = jnp.zeros(from_e.shape[:-1] + (LANES - blocks[0].shape[-1] - 2 * WIDE,), jnp.float32)
    return north, south, jnp.concatenate([from_e, gap, from_w], axis=-1)


def stencil_kernel(tr_ref, u_ref, v_ref, m_ref, f_ref, hn_ref, hs_ref, hc_ref, fn_ref, fs_ref, fc_ref,
                   o_ref, buf, uu, vv, mm, ff, cw, ce, cs, cn, cc, m8, mf):
    nt, nk, orows, ocols = tr_ref.shape
    _, planes, rows, lanes = buf.shape

    def place(dst, own, at):
        dst[:orows, :ocols] = own
        dst[orows:orows + WIDE, :ocols] = hn_ref[at]
        dst[orows + WIDE:, :ocols] = hs_ref[at]
        dst[:, ocols:] = hc_ref[at]

    def fill(p, carry):
        place(buf.at[0, p], tr_ref[p // nk, p % nk], p)
        return carry

    lax.fori_loop(0, planes, fill, 0)

    def fill_uv(k, carry):
        place(uu.at[k], u_ref[k].astype(jnp.float32), planes + k)
        place(vv.at[k], v_ref[k].astype(jnp.float32), planes + nk + k)
        return carry

    lax.fori_loop(0, nk, fill_uv, 0)
    place(mm, m_ref[...].astype(jnp.float32), planes + 2 * nk)
    for t in range(nt):
        ff[t, :orows, :ocols] = f_ref[t]
        ff[t, orows:orows + WIDE, :ocols] = fn_ref[t]
        ff[t, orows + WIDE:, :ocols] = fs_ref[t]
        ff[t, :, ocols:] = fc_ref[t]

    mask = mm[...]
    m8[...] = mask * 0.08
    for t in range(nt):
        mf[t] = mask * ff[t]

    def coef(k, carry):
        u = uu[k]
        v = vv[k]
        up = jnp.maximum(u, 0.0)
        um = jnp.minimum(u, 0.0)
        vp = jnp.maximum(v, 0.0)
        vm = jnp.minimum(v, 0.0)
        cw[k] = mask * (up + 0.08)
        ce[k] = mask * (0.08 - um)
        cs[k] = mask * (vp + 0.08)
        cn[k] = mask * (0.08 - vm)
        cc[k] = mask * ((um - up) + (vm - vp) - 0.48)
        return carry

    lax.fori_loop(0, nk, coef, 0)

    strips = rows // 8
    first_row = lax.broadcasted_iota(jnp.int32, (8, lanes), 0) == 0
    last_row = lax.broadcasted_iota(jnp.int32, (8, lanes), 0) == 7

    def plane(src, dst, k, above, below, forced):
        for i in range(strips):
            at = pl.ds(i * 8, 8)
            before = pl.ds((i - 1) % strips * 8, 8)
            after = pl.ds((i + 1) % strips * 8, 8)
            c_w = cw[k, at, :]
            c_e = ce[k, at, :]
            c_s = cs[k, at, :]
            c_n = cn[k, at, :]
            c_c = cc[k, at, :]
            c_8 = m8[at, :]
            for t in range(nt):
                p = t * nk + k
                cur = buf[src, p, at, :]
                south = jnp.where(first_row, pltpu.roll(buf[src, p, before, :], 1, 0), pltpu.roll(cur, 1, 0))
                north = jnp.where(last_row, pltpu.roll(buf[src, p, after, :], 7, 0), pltpu.roll(cur, 7, 0))
                west = pltpu.roll(cur, 1, 1)
                east = pltpu.roll(cur, lanes - 1, 1)
                up = cur if above is None else buf[src, t * nk + above, at, :]
                down = cur if below is None else buf[src, t * nk + below, at, :]
                tend = c_w * west + c_e * east + c_s * south + c_n * north + c_c * cur
                tend = tend + c_8 * (up + down)
                if forced:
                    tend = tend + mf[t, at, :]
                buf[dst, p, at, :] = cur + tend

    def step(i, carry):
        for src in (0, 1):
            dst = 1 - src
            for k in range(nk):
                plane(src, dst, k, k - 1 if k > 0 else None, k + 1 if k < nk - 1 else None, k == 0)
        return carry

    lax.fori_loop(0, STEPS // 2, step, 0)

    def out(p, carry):
        o_ref[p // nk, p % nk] = buf[STEPS % 2, p, :orows, :ocols]
        return carry

    lax.fori_loop(0, planes, out, 0)


def evolve(tracers, u_vel, v_vel, land_mask, forcing, halo, f_halo):
    nt, nk, orows, ocols = tracers.shape
    plane = (orows + 2 * WIDE, LANES)
    vm = lambda *shape: pltpu.VMEM(shape, jnp.float32)
    return pl.pallas_call(
        stencil_kernel,
        out_shape=jax.ShapeDtypeStruct(tracers.shape, jnp.float32),
        scratch_shapes=[
            vm(2, nt * nk, *plane),
            vm(nk, *plane),
            vm(nk, *plane),
            vm(*plane),
            vm(nt, *plane),
            vm(nk, *plane),
            vm(nk, *plane),
            vm(nk, *plane),
            vm(nk, *plane),
            vm(nk, *plane),
            vm(*plane),
            vm(nt, *plane),
        ],
        compiler_params=pltpu.CompilerParams(vmem_limit_bytes=62 * 1024 * 1024),
    )(tracers, u_vel, v_vel, land_mask, forcing, *halo, *f_halo)


def atmosphere_block(atm_flux):
    cols_n = lax.axis_size("ox")
    rows_n = lax.axis_size("oy")
    width = atm_flux.shape[2] // cols_n
    ring = jnp.concatenate([atm_flux[..., -H:], atm_flux, atm_flux[..., :H]], axis=2)
    pieces = jnp.stack([ring[..., i * width:(i + 1) * width + 2 * H] for i in range(cols_n)])
    got = lax.all_to_all(pieces, "ox", split_axis=0, concat_axis=0, tiled=True)
    own = jnp.concatenate(list(got), axis=1)
    below = lax.ppermute(own[:, -H:], "oy", [(i, i + 1) for i in range(rows_n - 1)])
    above = lax.ppermute(own[:, :H], "oy", [(i + 1, i) for i in range(rows_n - 1)])
    return jnp.concatenate([below, own, above], axis=1)


def remap(padded, remap_index, remap_weight):
    nf, arows, acols = padded.shape
    kk, orows, ocols = remap_index.shape
    base_r = jnp.arange(orows, dtype=jnp.int32) * (arows - 2 * H - 1) // (orows - 1) + H
    base_c = jnp.arange(ocols, dtype=jnp.int32) * (acols - 2 * H - 1) // (ocols - 1) + H
    offs = jnp.arange(2 * H + 1, dtype=jnp.int32) - H
    pick_r = (
        (base_r[None, :, None] + offs[:, None, None])
        == jnp.arange(arows, dtype=jnp.int32)[None, None, :]
    ).astype(jnp.float32).reshape(-1, arows)
    pick_c = (
        jnp.arange(acols, dtype=jnp.int32)[:, None, None]
        == (base_c[None, None, :] + offs[None, :, None])
    ).astype(jnp.float32).reshape(acols, -1)
    lifted = jnp.einsum("pa,fab->fpb", pick_r, padded, precision=HIGH)
    window = jnp.einsum("fpb,bq->fpq", lifted, pick_c, precision=HIGH)
    window = window.reshape(nf, 2 * H + 1, orows, 2 * H + 1, ocols)
    row_of = remap_index // acols - base_r[None, :, None] + H
    col_of = remap_index % acols - base_c[None, None, :] + H
    inside = (row_of >= 0) & (row_of <= 2 * H) & (col_of >= 0) & (col_of <= 2 * H)
    slot = jnp.where(inside, row_of * (2 * H + 1) + col_of, -1)
    slots = jnp.arange((2 * H + 1) ** 2, dtype=jnp.int32)
    wsum = jnp.sum(
        jnp.where(slot[:, None] == slots[None, :, None, None], remap_weight[:, None], 0.0),
        axis=0,
    ).reshape(2 * H + 1, 2 * H + 1, orows, ocols)
    fast = jnp.sum(window * wsum.transpose(0, 2, 1, 3)[None], axis=(1, 3))
    missed = jnp.logical_not(jnp.all(inside))

    def general():
        flat = padded.reshape(nf, -1)
        total = jnp.zeros((nf,) + remap_index.shape[1:], jnp.float32)
        for source in range(kk):
            picked = jnp.take(flat, remap_index[source], axis=1)
            total = total + remap_weight[source][None] * picked
        return total

    return lax.cond(missed, general, lambda: fast)


def on_device(atm_flux, remap_index, remap_weight, coupling, land_mask, tracers, u_vel, v_vel):
    fields = [
        tracers.reshape((-1,) + tracers.shape[2:]),
        u_vel.astype(jnp.float32),
        v_vel.astype(jnp.float32),
        land_mask.astype(jnp.float32)[None],
    ]
    halo = exchange(fields, [False, True, True, False])

    padded = atmosphere_block(atm_flux)
    ocean_flux = remap(padded, remap_index, remap_weight)
    forcing = jnp.sum(coupling[:, :, None, None] * ocean_flux[None], axis=1)
    f_halo = exchange([forcing], [False])
    final = evolve(tracers, u_vel, v_vel, land_mask, forcing, halo, f_halo)
    return (ocean_flux, final)


def solution(mesh):
    placed = (
        P(None, ("oy", "ox"), None),
        P(None, "oy", "ox"),
        P(None, "oy", "ox"),
        P(),
        P("oy", "ox"),
        P(None, None, "oy", "ox"),
        P(None, "oy", "ox"),
        P(None, "oy", "ox"),
    )
    return jax.shard_map(
        on_device,
        mesh=mesh,
        in_specs=placed,
        out_specs=(P(None, "oy", "ox"), P(None, None, "oy", "ox")),
        check_vma=False,
    )
```

```python
import jax
import jax.numpy as jnp
from jax import lax
from jax.sharding import PartitionSpec as P
from jax.experimental import pallas as pl
from jax.experimental.pallas import tpu as pltpu

H = 2
STEPS = 8
WIDE = 8
LANES = 384
HIGH = lax.Precision.HIGHEST


def with_halo(cells, sides, width, closed):
    for axis, dim in sides:
        count = lax.axis_size(axis)
        ends = count if closed else count - 1
        head = lax.slice_in_dim(cells, 0, width, axis=dim)
        tail = lax.slice_in_dim(cells, cells.shape[dim] - width, cells.shape[dim], axis=dim)
        cells = jnp.concatenate(
            [
                lax.ppermute(tail, axis, [(i, (i + 1) % count) for i in range(ends)]),
                cells,
                lax.ppermute(head, axis, [((i + 1) % count, i) for i in range(ends)]),
            ],
            axis=dim,
        )
    return cells


def exchange(blocks, flips):
    rows_n = lax.axis_size("oy")
    cols_n = lax.axis_size("ox")
    on_top = lax.axis_index("oy") == rows_n - 1
    sizes = [b.shape[0] for b in blocks]
    sign = jnp.concatenate(
        [jnp.full((n,), -1.0 if neg else 1.0, jnp.float32) for n, neg in zip(sizes, flips)]
    )[:, None, None]
    tops = jnp.concatenate([b[:, -WIDE:, :] for b in blocks], axis=0)
    bots = jnp.concatenate([b[:, :WIDE, :] for b in blocks], axis=0)
    south = lax.ppermute(tops, "oy", [(i, i + 1) for i in range(rows_n - 1)])
    north = lax.ppermute(bots, "oy", [(i + 1, i) for i in range(rows_n - 1)])
    top_row = (rows_n - 1) * cols_n
    fold = lax.ppermute(
        tops,
        ("oy", "ox"),
        [(top_row + (cols_n // 2 - j) % cols_n, top_row + j) for j in range(cols_n)],
    )
    north = jnp.where(on_top, fold[:, ::-1, ::-1] * sign, north)
    easts = jnp.concatenate(
        [jnp.concatenate([b[..., -WIDE:] for b in blocks], axis=0), north[..., -WIDE:], south[..., -WIDE:]],
        axis=1,
    )
    wests = jnp.concatenate(
        [jnp.concatenate([b[..., :WIDE] for b in blocks], axis=0), north[..., :WIDE], south[..., :WIDE]],
        axis=1,
    )
    from_w = lax.ppermute(easts, "ox", [(i, (i + 1) % cols_n) for i in range(cols_n)])
    from_e = lax.ppermute(wests, "ox", [((i + 1) % cols_n, i) for i in range(cols_n)])
    gap = jnp.zeros(from_e.shape[:-1] + (LANES - blocks[0].shape[-1] - 2 * WIDE,), jnp.float32)
    return north, south, jnp.concatenate([from_e, gap, from_w], axis=-1)


def stencil_kernel(tr_ref, u_ref, v_ref, m_ref, f_ref, hn_ref, hs_ref, hc_ref, fn_ref, fs_ref, fc_ref,
                   o_ref, buf, uu, vv, mm, ff, cw, ce, cs, cn, cc, m8, mf):
    nt, nk, orows, ocols = tr_ref.shape
    _, planes, rows, lanes = buf.shape

    def place(dst, own, at):
        dst[:orows, :ocols] = own
        dst[orows:orows + WIDE, :ocols] = hn_ref[at]
        dst[orows + WIDE:, :ocols] = hs_ref[at]
        dst[:, ocols:] = hc_ref[at]

    def fill(p, carry):
        place(buf.at[0, p], tr_ref[p // nk, p % nk], p)
        return carry

    lax.fori_loop(0, planes, fill, 0)

    def fill_uv(k, carry):
        place(uu.at[k], u_ref[k].astype(jnp.float32), planes + k)
        place(vv.at[k], v_ref[k].astype(jnp.float32), planes + nk + k)
        return carry

    lax.fori_loop(0, nk, fill_uv, 0)
    place(mm, m_ref[...].astype(jnp.float32), planes + 2 * nk)
    for t in range(nt):
        ff[t, :orows, :ocols] = f_ref[t]
        ff[t, orows:orows + WIDE, :ocols] = fn_ref[t]
        ff[t, orows + WIDE:, :ocols] = fs_ref[t]
        ff[t, :, ocols:] = fc_ref[t]

    mask = mm[...]
    m8[...] = mask * 0.08
    for t in range(nt):
        mf[t] = mask * ff[t]

    def coef(k, carry):
        u = uu[k]
        v = vv[k]
        up = jnp.maximum(u, 0.0)
        um = jnp.minimum(u, 0.0)
        vp = jnp.maximum(v, 0.0)
        vm = jnp.minimum(v, 0.0)
        cw[k] = mask * (up + 0.08)
        ce[k] = mask * (0.08 - um)
        cs[k] = mask * (vp + 0.08)
        cn[k] = mask * (0.08 - vm)
        cc[k] = mask * ((um - up) + (vm - vp) - 0.48)
        return carry

    lax.fori_loop(0, nk, coef, 0)

    strips = rows // 8
    first_row = lax.broadcasted_iota(jnp.int32, (8, lanes), 0) == 0
    last_row = lax.broadcasted_iota(jnp.int32, (8, lanes), 0) == 7

    def plane(src, dst, k, above, below, forced):
        for i in range(strips):
            at = pl.ds(i * 8, 8)
            before = pl.ds((i - 1) % strips * 8, 8)
            after = pl.ds((i + 1) % strips * 8, 8)
            c_w = cw[k, at, :]
            c_e = ce[k, at, :]
            c_s = cs[k, at, :]
            c_n = cn[k, at, :]
            c_c = cc[k, at, :]
            c_8 = m8[at, :]
            for t in range(nt):
                p = t * nk + k
                cur = buf[src, p, at, :]
                south = jnp.where(first_row, pltpu.roll(buf[src, p, before, :], 1, 0), pltpu.roll(cur, 1, 0))
                north = jnp.where(last_row, pltpu.roll(buf[src, p, after, :], 7, 0), pltpu.roll(cur, 7, 0))
                west = pltpu.roll(cur, 1, 1)
                east = pltpu.roll(cur, lanes - 1, 1)
                up = cur if above is None else buf[src, t * nk + above, at, :]
                down = cur if below is None else buf[src, t * nk + below, at, :]
                tend = c_w * west + c_e * east + c_s * south + c_n * north + c_c * cur
                tend = tend + c_8 * (up + down)
                if forced:
                    tend = tend + mf[t, at, :]
                buf[dst, p, at, :] = cur + tend

    def step(i, carry):
        for src in (0, 1):
            dst = 1 - src
            for k in range(nk):
                plane(src, dst, k, k - 1 if k > 0 else None, k + 1 if k < nk - 1 else None, k == 0)
        return carry

    lax.fori_loop(0, STEPS // 2, step, 0)

    def out(p, carry):
        o_ref[p // nk, p % nk] = buf[STEPS % 2, p, :orows, :ocols]
        return carry

    lax.fori_loop(0, planes, out, 0)


def evolve(tracers, u_vel, v_vel, land_mask, forcing, halo, f_halo):
    nt, nk, orows, ocols = tracers.shape
    plane = (orows + 2 * WIDE, LANES)
    vm = lambda *shape: pltpu.VMEM(shape, jnp.float32)
    return pl.pallas_call(
        stencil_kernel,
        out_shape=jax.ShapeDtypeStruct(tracers.shape, jnp.float32),
        scratch_shapes=[
            vm(2, nt * nk, *plane),
            vm(nk, *plane),
            vm(nk, *plane),
            vm(*plane),
            vm(nt, *plane),
            vm(nk, *plane),
            vm(nk, *plane),
            vm(nk, *plane),
            vm(nk, *plane),
            vm(nk, *plane),
            vm(*plane),
            vm(nt, *plane),
        ],
        compiler_params=pltpu.CompilerParams(vmem_limit_bytes=62 * 1024 * 1024),
    )(tracers, u_vel, v_vel, land_mask, forcing, *halo, *f_halo)


def atmosphere_block(atm_flux):
    cols_n = lax.axis_size("ox")
    rows_n = lax.axis_size("oy")
    width = atm_flux.shape[2] // cols_n
    nf, lat = atm_flux.shape[:2]
    body = jnp.roll(atm_flux, H, axis=2).reshape(nf, lat, cols_n, width)
    tail = jnp.roll(atm_flux, H - width, axis=2).reshape(nf, lat, cols_n, width)[..., : 2 * H]
    pieces = jnp.concatenate([body, tail], axis=3)
    got = lax.all_to_all(pieces, "ox", split_axis=2, concat_axis=1, tiled=True)
    own = got.reshape(nf, -1, width + 2 * H)
    below = lax.ppermute(own[:, -H:], "oy", [(i, i + 1) for i in range(rows_n - 1)])
    above = lax.ppermute(own[:, :H], "oy", [(i + 1, i) for i in range(rows_n - 1)])
    return jnp.concatenate([below, own, above], axis=1)


def remap(padded, remap_index, remap_weight):
    nf, arows, acols = padded.shape
    kk, orows, ocols = remap_index.shape
    base_r = jnp.arange(orows, dtype=jnp.int32) * (arows - 2 * H - 1) // (orows - 1) + H
    base_c = jnp.arange(ocols, dtype=jnp.int32) * (acols - 2 * H - 1) // (ocols - 1) + H
    offs = jnp.arange(2 * H + 1, dtype=jnp.int32) - H
    pick_r = (
        (base_r[None, :, None] + offs[:, None, None])
        == jnp.arange(arows, dtype=jnp.int32)[None, None, :]
    ).astype(jnp.float32).reshape(-1, arows)
    pick_c = (
        jnp.arange(acols, dtype=jnp.int32)[:, None, None]
        == (base_c[None, None, :] + offs[None, :, None])
    ).astype(jnp.float32).reshape(acols, -1)
    lifted = jnp.einsum("pa,fab->fpb", pick_r, padded, precision=HIGH)
    window = jnp.einsum("fpb,bq->fpq", lifted, pick_c, precision=HIGH)
    window = window.reshape(nf, 2 * H + 1, orows, 2 * H + 1, ocols)
    row_of = remap_index // acols - base_r[None, :, None] + H
    col_of = remap_index % acols - base_c[None, None, :] + H
    inside = (row_of >= 0) & (row_of <= 2 * H) & (col_of >= 0) & (col_of <= 2 * H)
    slot = jnp.where(inside, row_of * (2 * H + 1) + col_of, -1)
    slots = jnp.arange((2 * H + 1) ** 2, dtype=jnp.int32)
    wsum = jnp.sum(
        jnp.where(slot[:, None] == slots[None, :, None, None], remap_weight[:, None], 0.0),
        axis=0,
    ).reshape(2 * H + 1, 2 * H + 1, orows, ocols)
    fast = jnp.sum(window * wsum.transpose(0, 2, 1, 3)[None], axis=(1, 3))
    missed = jnp.logical_not(jnp.all(inside))

    def general():
        flat = padded.reshape(nf, -1)
        total = jnp.zeros((nf,) + remap_index.shape[1:], jnp.float32)
        for source in range(kk):
            picked = jnp.take(flat, remap_index[source], axis=1)
            total = total + remap_weight[source][None] * picked
        return total

    return lax.cond(missed, general, lambda: fast)


def on_device(atm_flux, remap_index, remap_weight, coupling, land_mask, tracers, u_vel, v_vel):
    fields = [
        tracers.reshape((-1,) + tracers.shape[2:]),
        u_vel.astype(jnp.float32),
        v_vel.astype(jnp.float32),
        land_mask.astype(jnp.float32)[None],
    ]
    halo = exchange(fields, [False, True, True, False])

    padded = atmosphere_block(atm_flux)
    ocean_flux = remap(padded, remap_index, remap_weight)
    forcing = jnp.sum(coupling[:, :, None, None] * ocean_flux[None], axis=1)
    f_halo = exchange([forcing], [False])
    final = evolve(tracers, u_vel, v_vel, land_mask, forcing, halo, f_halo)
    return (ocean_flux, final)


def solution(mesh):
    placed = (
        P(None, ("oy", "ox"), None),
        P(None, "oy", "ox"),
        P(None, "oy", "ox"),
        P(),
        P("oy", "ox"),
        P(None, None, "oy", "ox"),
        P(None, "oy", "ox"),
        P(None, "oy", "ox"),
    )
    return jax.shard_map(
        on_device,
        mesh=mesh,
        in_specs=placed,
        out_specs=(P(None, "oy", "ox"), P(None, None, "oy", "ox")),
        check_vma=False,
    )
```

```python
import jax
import jax.numpy as jnp
from jax import lax
from jax.sharding import PartitionSpec as P
from jax.experimental import pallas as pl
from jax.experimental.pallas import tpu as pltpu

H = 2
STEPS = 8
WIDE = 8
LANES = 384
HIGH = lax.Precision.HIGHEST


def with_halo(cells, sides, width, closed):
    for axis, dim in sides:
        count = lax.axis_size(axis)
        ends = count if closed else count - 1
        head = lax.slice_in_dim(cells, 0, width, axis=dim)
        tail = lax.slice_in_dim(cells, cells.shape[dim] - width, cells.shape[dim], axis=dim)
        cells = jnp.concatenate(
            [
                lax.ppermute(tail, axis, [(i, (i + 1) % count) for i in range(ends)]),
                cells,
                lax.ppermute(head, axis, [((i + 1) % count, i) for i in range(ends)]),
            ],
            axis=dim,
        )
    return cells


def exchange(blocks, flips):
    rows_n = lax.axis_size("oy")
    cols_n = lax.axis_size("ox")
    on_top = lax.axis_index("oy") == rows_n - 1
    sizes = [b.shape[0] for b in blocks]
    sign = jnp.concatenate(
        [jnp.full((n,), -1.0 if neg else 1.0, jnp.float32) for n, neg in zip(sizes, flips)]
    )[:, None, None]
    tops = jnp.concatenate([b[:, -WIDE:, :] for b in blocks], axis=0)
    bots = jnp.concatenate([b[:, :WIDE, :] for b in blocks], axis=0)
    south = lax.ppermute(tops, "oy", [(i, i + 1) for i in range(rows_n - 1)])
    north = lax.ppermute(bots, "oy", [(i + 1, i) for i in range(rows_n - 1)])
    top_row = (rows_n - 1) * cols_n
    fold = lax.ppermute(
        tops,
        ("oy", "ox"),
        [(top_row + (cols_n // 2 - j) % cols_n, top_row + j) for j in range(cols_n)],
    )
    north = jnp.where(on_top, fold[:, ::-1, ::-1] * sign, north)
    easts = jnp.concatenate(
        [jnp.concatenate([b[..., -WIDE:] for b in blocks], axis=0), north[..., -WIDE:], south[..., -WIDE:]],
        axis=1,
    )
    wests = jnp.concatenate(
        [jnp.concatenate([b[..., :WIDE] for b in blocks], axis=0), north[..., :WIDE], south[..., :WIDE]],
        axis=1,
    )
    from_w = lax.ppermute(easts, "ox", [(i, (i + 1) % cols_n) for i in range(cols_n)])
    from_e = lax.ppermute(wests, "ox", [((i + 1) % cols_n, i) for i in range(cols_n)])
    gap = jnp.zeros(from_e.shape[:-1] + (LANES - blocks[0].shape[-1] - 2 * WIDE,), jnp.float32)
    return north, south, jnp.concatenate([from_e, gap, from_w], axis=-1)


def stencil_kernel(tr_ref, u_ref, v_ref, m_ref, f_ref, hn_ref, hs_ref, hc_ref, fn_ref, fs_ref, fc_ref,
                   o_ref, buf, uu, vv, mm, ff, cw, ce, cs, cn, cc, m8, mf):
    nt, nk, orows, ocols = tr_ref.shape
    _, planes, rows, lanes = buf.shape

    def place(dst, own, at):
        dst[:orows, :ocols] = own
        dst[orows:orows + WIDE, :ocols] = hn_ref[at]
        dst[orows + WIDE:, :ocols] = hs_ref[at]
        dst[:, ocols:] = hc_ref[at]

    def fill(p, carry):
        place(buf.at[0, p], tr_ref[p // nk, p % nk], p)
        return carry

    lax.fori_loop(0, planes, fill, 0)

    def fill_uv(k, carry):
        place(uu.at[k], u_ref[k].astype(jnp.float32), planes + k)
        place(vv.at[k], v_ref[k].astype(jnp.float32), planes + nk + k)
        return carry

    lax.fori_loop(0, nk, fill_uv, 0)
    place(mm, m_ref[...].astype(jnp.float32), planes + 2 * nk)
    for t in range(nt):
        ff[t, :orows, :ocols] = f_ref[t]
        ff[t, orows:orows + WIDE, :ocols] = fn_ref[t]
        ff[t, orows + WIDE:, :ocols] = fs_ref[t]
        ff[t, :, ocols:] = fc_ref[t]

    mask = mm[...]
    m8[...] = mask * 0.08
    for t in range(nt):
        mf[t] = mask * ff[t]

    def coef(k, carry):
        u = uu[k]
        v = vv[k]
        up = jnp.maximum(u, 0.0)
        um = jnp.minimum(u, 0.0)
        vp = jnp.maximum(v, 0.0)
        vm = jnp.minimum(v, 0.0)
        cw[k] = mask * (up + 0.08)
        ce[k] = mask * (0.08 - um)
        cs[k] = mask * (vp + 0.08)
        cn[k] = mask * (0.08 - vm)
        cc[k] = mask * ((um - up) + (vm - vp) - 0.48)
        return carry

    lax.fori_loop(0, nk, coef, 0)

    strips = rows // 8
    first_row = lax.broadcasted_iota(jnp.int32, (8, lanes), 0) == 0
    last_row = lax.broadcasted_iota(jnp.int32, (8, lanes), 0) == 7

    def plane(src, dst, k, above, below, forced):
        for i in range(strips):
            at = pl.ds(i * 8, 8)
            before = pl.ds((i - 1) % strips * 8, 8)
            after = pl.ds((i + 1) % strips * 8, 8)
            c_w = cw[k, at, :]
            c_e = ce[k, at, :]
            c_s = cs[k, at, :]
            c_n = cn[k, at, :]
            c_c = cc[k, at, :]
            c_8 = m8[at, :]
            for t in range(nt):
                p = t * nk + k
                cur = buf[src, p, at, :]
                south = jnp.where(first_row, pltpu.roll(buf[src, p, before, :], 1, 0), pltpu.roll(cur, 1, 0))
                north = jnp.where(last_row, pltpu.roll(buf[src, p, after, :], 7, 0), pltpu.roll(cur, 7, 0))
                west = pltpu.roll(cur, 1, 1)
                east = pltpu.roll(cur, lanes - 1, 1)
                up = cur if above is None else buf[src, t * nk + above, at, :]
                down = cur if below is None else buf[src, t * nk + below, at, :]
                tend = c_w * west + c_e * east + c_s * south + c_n * north + c_c * cur
                tend = tend + c_8 * (up + down)
                if forced:
                    tend = tend + mf[t, at, :]
                buf[dst, p, at, :] = cur + tend

    def step(i, carry):
        for src in (0, 1):
            dst = 1 - src
            for k in range(nk):
                plane(src, dst, k, k - 1 if k > 0 else None, k + 1 if k < nk - 1 else None, k == 0)
        return carry

    lax.fori_loop(0, STEPS // 2, step, 0)

    def out(p, carry):
        o_ref[p // nk, p % nk] = buf[STEPS % 2, p, :orows, :ocols]
        return carry

    lax.fori_loop(0, planes, out, 0)


def evolve(tracers, u_vel, v_vel, land_mask, forcing, halo, f_halo):
    nt, nk, orows, ocols = tracers.shape
    plane = (orows + 2 * WIDE, LANES)
    vm = lambda *shape: pltpu.VMEM(shape, jnp.float32)
    return pl.pallas_call(
        stencil_kernel,
        out_shape=jax.ShapeDtypeStruct(tracers.shape, jnp.float32),
        scratch_shapes=[
            vm(2, nt * nk, *plane),
            vm(nk, *plane),
            vm(nk, *plane),
            vm(*plane),
            vm(nt, *plane),
            vm(nk, *plane),
            vm(nk, *plane),
            vm(nk, *plane),
            vm(nk, *plane),
            vm(nk, *plane),
            vm(*plane),
            vm(nt, *plane),
        ],
        compiler_params=pltpu.CompilerParams(vmem_limit_bytes=62 * 1024 * 1024),
    )(tracers, u_vel, v_vel, land_mask, forcing, *halo, *f_halo)


def atmosphere_block(atm_flux):
    cols_n = lax.axis_size("ox")
    rows_n = lax.axis_size("oy")
    width = atm_flux.shape[2] // cols_n
    nf, lat = atm_flux.shape[:2]
    body = jnp.roll(atm_flux, H, axis=2).reshape(nf, lat, cols_n, width)
    tail = jnp.roll(atm_flux, H - width, axis=2).reshape(nf, lat, cols_n, width)[..., : 2 * H]
    pieces = jnp.concatenate([body, tail], axis=3)
    got = lax.all_to_all(pieces, "ox", split_axis=2, concat_axis=1, tiled=True)
    own = got.reshape(nf, -1, width + 2 * H)
    below = lax.ppermute(own[:, -H:], "oy", [(i, i + 1) for i in range(rows_n - 1)])
    above = lax.ppermute(own[:, :H], "oy", [(i + 1, i) for i in range(rows_n - 1)])
    return jnp.concatenate([below, own, above], axis=1)


def remap(padded, remap_index, remap_weight):
    nf, arows, acols = padded.shape
    kk, orows, ocols = remap_index.shape
    base_r = jnp.arange(orows, dtype=jnp.int32) * (arows - 2 * H - 1) // (orows - 1) + H
    base_c = jnp.arange(ocols, dtype=jnp.int32) * (acols - 2 * H - 1) // (ocols - 1) + H
    offs = jnp.arange(2 * H + 1, dtype=jnp.int32) - H
    pick_r = (
        (base_r[None, :, None] + offs[:, None, None])
        == jnp.arange(arows, dtype=jnp.int32)[None, None, :]
    ).astype(jnp.float32).reshape(-1, arows)
    pick_c = (
        jnp.arange(acols, dtype=jnp.int32)[:, None, None]
        == (base_c[None, None, :] + offs[None, :, None])
    ).astype(jnp.float32).reshape(acols, -1)
    lifted = jnp.einsum("pa,fab->fpb", pick_r, padded, precision=HIGH)
    window = jnp.einsum("fpb,bq->fpq", lifted, pick_c, precision=HIGH)
    window = window.reshape(nf, 2 * H + 1, orows, 2 * H + 1, ocols)
    row_of = remap_index // acols - base_r[None, :, None] + H
    col_of = remap_index % acols - base_c[None, None, :] + H
    inside = (row_of >= 0) & (row_of <= 2 * H) & (col_of >= 0) & (col_of <= 2 * H)
    slot = jnp.where(inside, row_of * (2 * H + 1) + col_of, -1)
    slots = jnp.arange((2 * H + 1) ** 2, dtype=jnp.int32)
    wsum = jnp.sum(
        jnp.where(slot[:, None] == slots[None, :, None, None], remap_weight[:, None], 0.0),
        axis=0,
    ).reshape(2 * H + 1, 2 * H + 1, orows, ocols)
    fast = jnp.sum(window * wsum.transpose(0, 2, 1, 3)[None], axis=(1, 3))
    missed = jnp.logical_not(jnp.all(inside))

    def general():
        flat = padded.reshape(nf, -1)
        total = jnp.zeros((nf,) + remap_index.shape[1:], jnp.float32)
        for source in range(kk):
            picked = jnp.take(flat, remap_index[source], axis=1)
            total = total + remap_weight[source][None] * picked
        return total

    return lax.cond(missed, general, lambda: fast)


def on_device(atm_flux, remap_index, remap_weight, coupling, land_mask, tracers, u_vel, v_vel):
    fields = [
        tracers.reshape((-1,) + tracers.shape[2:]),
        u_vel.astype(jnp.float32),
        v_vel.astype(jnp.float32),
        land_mask.astype(jnp.float32)[None],
    ]
    halo = exchange(fields, [False, True, True, False])

    padded = atmosphere_block(atm_flux)
    halo, padded = lax.optimization_barrier((halo, padded))
    ocean_flux = remap(padded, remap_index, remap_weight)
    forcing = jnp.sum(coupling[:, :, None, None] * ocean_flux[None], axis=1)
    f_halo = exchange([forcing], [False])
    final = evolve(tracers, u_vel, v_vel, land_mask, forcing, halo, f_halo)
    return (ocean_flux, final)


def solution(mesh):
    placed = (
        P(None, ("oy", "ox"), None),
        P(None, "oy", "ox"),
        P(None, "oy", "ox"),
        P(),
        P("oy", "ox"),
        P(None, None, "oy", "ox"),
        P(None, "oy", "ox"),
        P(None, "oy", "ox"),
    )
    return jax.shard_map(
        on_device,
        mesh=mesh,
        in_specs=placed,
        out_specs=(P(None, "oy", "ox"), P(None, None, "oy", "ox")),
        check_vma=False,
    )
```

```python
import functools

import jax
import jax.numpy as jnp
from jax import lax
from jax.sharding import PartitionSpec as P
from jax.experimental import pallas as pl
from jax.experimental.pallas import tpu as pltpu

H = 2
STEPS = 8
WIDE = 8
LANES = 384
HIGH = lax.Precision.HIGHEST


def with_halo(cells, sides, width, closed):
    for axis, dim in sides:
        count = lax.axis_size(axis)
        ends = count if closed else count - 1
        head = lax.slice_in_dim(cells, 0, width, axis=dim)
        tail = lax.slice_in_dim(cells, cells.shape[dim] - width, cells.shape[dim], axis=dim)
        cells = jnp.concatenate(
            [
                lax.ppermute(tail, axis, [(i, (i + 1) % count) for i in range(ends)]),
                cells,
                lax.ppermute(head, axis, [((i + 1) % count, i) for i in range(ends)]),
            ],
            axis=dim,
        )
    return cells


def exchange(blocks, flips):
    rows_n = lax.axis_size("oy")
    cols_n = lax.axis_size("ox")
    on_top = lax.axis_index("oy") == rows_n - 1
    sizes = [b.shape[0] for b in blocks]
    sign = jnp.concatenate(
        [jnp.full((n,), -1.0 if neg else 1.0, jnp.float32) for n, neg in zip(sizes, flips)]
    )[:, None, None]
    tops = jnp.concatenate([b[:, -WIDE:, :] for b in blocks], axis=0)
    bots = jnp.concatenate([b[:, :WIDE, :] for b in blocks], axis=0)
    south = lax.ppermute(tops, "oy", [(i, i + 1) for i in range(rows_n - 1)])
    north = lax.ppermute(bots, "oy", [(i + 1, i) for i in range(rows_n - 1)])
    top_row = (rows_n - 1) * cols_n
    fold = lax.ppermute(
        tops,
        ("oy", "ox"),
        [(top_row + (cols_n // 2 - j) % cols_n, top_row + j) for j in range(cols_n)],
    )
    north = jnp.where(on_top, fold[:, ::-1, ::-1] * sign, north)
    easts = jnp.concatenate(
        [jnp.concatenate([b[..., -WIDE:] for b in blocks], axis=0), north[..., -WIDE:], south[..., -WIDE:]],
        axis=1,
    )
    wests = jnp.concatenate(
        [jnp.concatenate([b[..., :WIDE] for b in blocks], axis=0), north[..., :WIDE], south[..., :WIDE]],
        axis=1,
    )
    from_w = lax.ppermute(easts, "ox", [(i, (i + 1) % cols_n) for i in range(cols_n)])
    from_e = lax.ppermute(wests, "ox", [((i + 1) % cols_n, i) for i in range(cols_n)])
    gap = jnp.zeros(from_e.shape[:-1] + (LANES - blocks[0].shape[-1] - 2 * WIDE,), jnp.float32)
    return north, south, jnp.concatenate([from_e, gap, from_w], axis=-1)


def stencil_kernel(alone, tr_ref, u_ref, v_ref, m_ref, f_ref, hn_ref, hs_ref, hc_ref, fn_ref, fs_ref, fc_ref,
                   o_ref, buf, uu, vv, mm, ff, cw, ce, cs, cn, cc, m8, mf):
    nt, nk, orows, ocols = tr_ref.shape
    _, planes, rows, lanes = buf.shape

    def place(dst, own, at):
        dst[:orows, :ocols] = own
        dst[orows:orows + WIDE, :ocols] = hn_ref[at]
        dst[orows + WIDE:, :ocols] = hs_ref[at]
        dst[:, ocols:] = hc_ref[at]

    def fill(p, carry):
        if alone:
            buf[0, p] = jnp.zeros((rows, lanes), jnp.float32)
            buf[1, p] = jnp.zeros((rows, lanes), jnp.float32)
        else:
            place(buf.at[0, p], tr_ref[p // nk, p % nk], p)
        return carry

    lax.fori_loop(0, planes, fill, 0)

    def fill_uv(k, carry):
        place(uu.at[k], u_ref[k].astype(jnp.float32), planes + k)
        place(vv.at[k], v_ref[k].astype(jnp.float32), planes + nk + k)
        return carry

    lax.fori_loop(0, nk, fill_uv, 0)
    place(mm, m_ref[...].astype(jnp.float32), planes + 2 * nk)
    for t in range(nt):
        ff[t, :orows, :ocols] = f_ref[t]
        ff[t, orows:orows + WIDE, :ocols] = fn_ref[t]
        ff[t, orows + WIDE:, :ocols] = fs_ref[t]
        ff[t, :, ocols:] = fc_ref[t]

    mask = mm[...]
    m8[...] = mask * 0.08
    for t in range(nt):
        mf[t] = mask * ff[t]

    def coef(k, carry):
        u = uu[k]
        v = vv[k]
        up = jnp.maximum(u, 0.0)
        um = jnp.minimum(u, 0.0)
        vp = jnp.maximum(v, 0.0)
        vm = jnp.minimum(v, 0.0)
        cw[k] = mask * (up + 0.08)
        ce[k] = mask * (0.08 - um)
        cs[k] = mask * (vp + 0.08)
        cn[k] = mask * (0.08 - vm)
        cc[k] = mask * ((um - up) + (vm - vp) - 0.48)
        return carry

    lax.fori_loop(0, nk, coef, 0)

    strips = rows // 8
    first_row = lax.broadcasted_iota(jnp.int32, (8, lanes), 0) == 0
    last_row = lax.broadcasted_iota(jnp.int32, (8, lanes), 0) == 7

    def plane(src, dst, k, above, below, forced):
        for i in range(strips):
            at = pl.ds(i * 8, 8)
            before = pl.ds((i - 1) % strips * 8, 8)
            after = pl.ds((i + 1) % strips * 8, 8)
            c_w = cw[k, at, :]
            c_e = ce[k, at, :]
            c_s = cs[k, at, :]
            c_n = cn[k, at, :]
            c_c = cc[k, at, :]
            c_8 = m8[at, :]
            for t in range(nt):
                p = t * nk + k
                cur = buf[src, p, at, :]
                south = jnp.where(first_row, pltpu.roll(buf[src, p, before, :], 1, 0), pltpu.roll(cur, 1, 0))
                north = jnp.where(last_row, pltpu.roll(buf[src, p, after, :], 7, 0), pltpu.roll(cur, 7, 0))
                west = pltpu.roll(cur, 1, 1)
                east = pltpu.roll(cur, lanes - 1, 1)
                up = cur if above is None else buf[src, t * nk + above, at, :]
                down = cur if below is None else buf[src, t * nk + below, at, :]
                tend = c_w * west + c_e * east + c_s * south + c_n * north + c_c * cur
                tend = tend + c_8 * (up + down)
                if forced:
                    tend = tend + mf[t, at, :]
                buf[dst, p, at, :] = cur + tend

    def step(i, carry):
        for src in (0, 1):
            dst = 1 - src
            for k in range(nk):
                plane(src, dst, k, k - 1 if k > 0 else None, k + 1 if k < nk - 1 else None, k == 0)
        return carry

    if alone:
        for i in range(STEPS):
            for k in range(min(i + 1, nk)):
                plane(i % 2, 1 - i % 2, k, k - 1 if k > 0 else None, k + 1 if k < nk - 1 else None, k == 0)

        def out(p, carry):
            t = p // nk
            k = p % nk
            o_ref[t, k] = tr_ref[t, k] + buf[STEPS % 2, p, :orows, :ocols]
            return carry

        lax.fori_loop(0, planes, out, 0)
        return

    lax.fori_loop(0, STEPS // 2, step, 0)

    def out(p, carry):
        o_ref[p // nk, p % nk] = buf[STEPS % 2, p, :orows, :ocols]
        return carry

    lax.fori_loop(0, planes, out, 0)


def evolve(alone, tracers, u_vel, v_vel, land_mask, forcing, halo, f_halo):
    nt, nk, orows, ocols = tracers.shape
    plane = (orows + 2 * WIDE, LANES)
    vm = lambda *shape: pltpu.VMEM(shape, jnp.float32)
    return pl.pallas_call(
        functools.partial(stencil_kernel, alone),
        out_shape=jax.ShapeDtypeStruct(tracers.shape, jnp.float32),
        scratch_shapes=[
            vm(2, nt * nk, *plane),
            vm(nk, *plane),
            vm(nk, *plane),
            vm(*plane),
            vm(nt, *plane),
            vm(nk, *plane),
            vm(nk, *plane),
            vm(nk, *plane),
            vm(nk, *plane),
            vm(nk, *plane),
            vm(*plane),
            vm(nt, *plane),
        ],
        compiler_params=pltpu.CompilerParams(vmem_limit_bytes=62 * 1024 * 1024),
    )(tracers, u_vel, v_vel, land_mask, forcing, *halo, *f_halo)


def atmosphere_block(atm_flux):
    cols_n = lax.axis_size("ox")
    rows_n = lax.axis_size("oy")
    width = atm_flux.shape[2] // cols_n
    nf, lat = atm_flux.shape[:2]
    body = jnp.roll(atm_flux, H, axis=2).reshape(nf, lat, cols_n, width)
    tail = jnp.roll(atm_flux, H - width, axis=2).reshape(nf, lat, cols_n, width)[..., : 2 * H]
    pieces = jnp.concatenate([body, tail], axis=3)
    got = lax.all_to_all(pieces, "ox", split_axis=2, concat_axis=1, tiled=True)
    own = got.reshape(nf, -1, width + 2 * H)
    below = lax.ppermute(own[:, -H:], "oy", [(i, i + 1) for i in range(rows_n - 1)])
    above = lax.ppermute(own[:, :H], "oy", [(i + 1, i) for i in range(rows_n - 1)])
    return jnp.concatenate([below, own, above], axis=1)


def remap(padded, remap_index, remap_weight):
    nf, arows, acols = padded.shape
    kk, orows, ocols = remap_index.shape
    base_r = jnp.arange(orows, dtype=jnp.int32) * (arows - 2 * H - 1) // (orows - 1) + H
    base_c = jnp.arange(ocols, dtype=jnp.int32) * (acols - 2 * H - 1) // (ocols - 1) + H
    offs = jnp.arange(2 * H + 1, dtype=jnp.int32) - H
    pick_r = (
        (base_r[None, :, None] + offs[:, None, None])
        == jnp.arange(arows, dtype=jnp.int32)[None, None, :]
    ).astype(jnp.float32).reshape(-1, arows)
    pick_c = (
        jnp.arange(acols, dtype=jnp.int32)[:, None, None]
        == (base_c[None, None, :] + offs[None, :, None])
    ).astype(jnp.float32).reshape(acols, -1)
    lifted = jnp.einsum("pa,fab->fpb", pick_r, padded, precision=HIGH)
    window = jnp.einsum("fpb,bq->fpq", lifted, pick_c, precision=HIGH)
    window = window.reshape(nf, 2 * H + 1, orows, 2 * H + 1, ocols)
    row_of = remap_index // acols - base_r[None, :, None] + H
    col_of = remap_index % acols - base_c[None, None, :] + H
    inside = (row_of >= 0) & (row_of <= 2 * H) & (col_of >= 0) & (col_of <= 2 * H)
    slot = jnp.where(inside, row_of * (2 * H + 1) + col_of, -1)
    slots = jnp.arange((2 * H + 1) ** 2, dtype=jnp.int32)
    wsum = jnp.sum(
        jnp.where(slot[:, None] == slots[None, :, None, None], remap_weight[:, None], 0.0),
        axis=0,
    ).reshape(2 * H + 1, 2 * H + 1, orows, ocols)
    fast = jnp.sum(window * wsum.transpose(0, 2, 1, 3)[None], axis=(1, 3))
    missed = jnp.logical_not(jnp.all(inside))

    def general():
        flat = padded.reshape(nf, -1)
        total = jnp.zeros((nf,) + remap_index.shape[1:], jnp.float32)
        for source in range(kk):
            picked = jnp.take(flat, remap_index[source], axis=1)
            total = total + remap_weight[source][None] * picked
        return total

    return lax.cond(missed, general, lambda: fast)


def on_device(atm_flux, remap_index, remap_weight, coupling, land_mask, tracers, u_vel, v_vel):
    fields = [
        tracers.reshape((-1,) + tracers.shape[2:]),
        u_vel.astype(jnp.float32),
        v_vel.astype(jnp.float32),
        land_mask.astype(jnp.float32)[None],
    ]
    halo = exchange(fields, [False, True, True, False])

    padded = atmosphere_block(atm_flux)
    halo, padded = lax.optimization_barrier((halo, padded))
    ocean_flux = remap(padded, remap_index, remap_weight)
    forcing = jnp.sum(coupling[:, :, None, None] * ocean_flux[None], axis=1)
    nt, orows, ocols = forcing.shape
    no_halo = (
        jnp.zeros((nt, WIDE, ocols), jnp.float32),
        jnp.zeros((nt, WIDE, ocols), jnp.float32),
        jnp.zeros((nt, orows + 2 * WIDE, LANES - ocols), jnp.float32),
    )
    own = evolve(False, tracers, u_vel, v_vel, land_mask, forcing, halo, no_halo)
    f_halo = exchange([forcing], [False])
    final = evolve(True, own, u_vel, v_vel, land_mask, jnp.zeros_like(forcing), halo, f_halo)
    return (ocean_flux, final)


def solution(mesh):
    placed = (
        P(None, ("oy", "ox"), None),
        P(None, "oy", "ox"),
        P(None, "oy", "ox"),
        P(),
        P("oy", "ox"),
        P(None, None, "oy", "ox"),
        P(None, "oy", "ox"),
        P(None, "oy", "ox"),
    )
    return jax.shard_map(
        on_device,
        mesh=mesh,
        in_specs=placed,
        out_specs=(P(None, "oy", "ox"), P(None, None, "oy", "ox")),
        check_vma=False,
    )
```

```python
import jax
import jax.numpy as jnp
from jax import lax
from jax.sharding import PartitionSpec as P
from jax.experimental import pallas as pl
from jax.experimental.pallas import tpu as pltpu

H = 2
STEPS = 8
WIDE = 8
LANES = 384
HIGH = lax.Precision.HIGHEST


def with_halo(cells, sides, width, closed):
    for axis, dim in sides:
        count = lax.axis_size(axis)
        ends = count if closed else count - 1
        head = lax.slice_in_dim(cells, 0, width, axis=dim)
        tail = lax.slice_in_dim(cells, cells.shape[dim] - width, cells.shape[dim], axis=dim)
        cells = jnp.concatenate(
            [
                lax.ppermute(tail, axis, [(i, (i + 1) % count) for i in range(ends)]),
                cells,
                lax.ppermute(head, axis, [((i + 1) % count, i) for i in range(ends)]),
            ],
            axis=dim,
        )
    return cells


def exchange(blocks, flips):
    rows_n = lax.axis_size("oy")
    cols_n = lax.axis_size("ox")
    on_top = lax.axis_index("oy") == rows_n - 1
    sizes = [b.shape[0] for b in blocks]
    sign = jnp.concatenate(
        [jnp.full((n,), -1.0 if neg else 1.0, jnp.float32) for n, neg in zip(sizes, flips)]
    )[:, None, None]
    tops = jnp.concatenate([b[:, -WIDE:, :] for b in blocks], axis=0)
    bots = jnp.concatenate([b[:, :WIDE, :] for b in blocks], axis=0)
    south = lax.ppermute(tops, "oy", [(i, i + 1) for i in range(rows_n - 1)])
    north = lax.ppermute(bots, "oy", [(i + 1, i) for i in range(rows_n - 1)])
    top_row = (rows_n - 1) * cols_n
    fold = lax.ppermute(
        tops,
        ("oy", "ox"),
        [(top_row + (cols_n // 2 - j) % cols_n, top_row + j) for j in range(cols_n)],
    )
    north = jnp.where(on_top, fold[:, ::-1, ::-1] * sign, north)
    easts = jnp.concatenate(
        [jnp.concatenate([b[..., -WIDE:] for b in blocks], axis=0), north[..., -WIDE:], south[..., -WIDE:]],
        axis=1,
    )
    wests = jnp.concatenate(
        [jnp.concatenate([b[..., :WIDE] for b in blocks], axis=0), north[..., :WIDE], south[..., :WIDE]],
        axis=1,
    )
    from_w = lax.ppermute(easts, "ox", [(i, (i + 1) % cols_n) for i in range(cols_n)])
    from_e = lax.ppermute(wests, "ox", [((i + 1) % cols_n, i) for i in range(cols_n)])
    return north, south, (from_e, from_w)


def lane_tile(sides, cols):
    from_e, from_w = sides
    gap = jnp.zeros(from_e.shape[:-1] + (LANES - cols - 2 * WIDE,), jnp.float32)
    return jnp.concatenate([from_e, gap, from_w], axis=-1)


def stencil_kernel(tr_ref, u_ref, v_ref, m_ref, f_ref, hn_ref, hs_ref, hc_ref, fn_ref, fs_ref, fc_ref,
                   o_ref, buf, uu, vv, mm, ff, cw, ce, cs, cn, cc, m8, mf):
    nt, nk, orows, ocols = tr_ref.shape
    _, planes, rows, lanes = buf.shape

    def place(dst, own, at):
        dst[:orows, :ocols] = own
        dst[orows:orows + WIDE, :ocols] = hn_ref[at]
        dst[orows + WIDE:, :ocols] = hs_ref[at]
        dst[:, ocols:] = hc_ref[at]

    def fill(p, carry):
        place(buf.at[0, p], tr_ref[p // nk, p % nk], p)
        return carry

    lax.fori_loop(0, planes, fill, 0)

    def fill_uv(k, carry):
        place(uu.at[k], u_ref[k].astype(jnp.float32), planes + k)
        place(vv.at[k], v_ref[k].astype(jnp.float32), planes + nk + k)
        return carry

    lax.fori_loop(0, nk, fill_uv, 0)
    place(mm, m_ref[...].astype(jnp.float32), planes + 2 * nk)
    for t in range(nt):
        ff[t, :orows, :ocols] = f_ref[t]
        ff[t, orows:orows + WIDE, :ocols] = fn_ref[t]
        ff[t, orows + WIDE:, :ocols] = fs_ref[t]
        ff[t, :, ocols:] = fc_ref[t]

    mask = mm[...]
    m8[...] = mask * 0.08
    for t in range(nt):
        mf[t] = mask * ff[t]

    def coef(k, carry):
        u = uu[k]
        v = vv[k]
        up = jnp.maximum(u, 0.0)
        um = jnp.minimum(u, 0.0)
        vp = jnp.maximum(v, 0.0)
        vm = jnp.minimum(v, 0.0)
        cw[k] = mask * (up + 0.08)
        ce[k] = mask * (0.08 - um)
        cs[k] = mask * (vp + 0.08)
        cn[k] = mask * (0.08 - vm)
        cc[k] = mask * ((um - up) + (vm - vp) - 0.48)
        return carry

    lax.fori_loop(0, nk, coef, 0)

    strips = rows // 8
    first_row = lax.broadcasted_iota(jnp.int32, (8, lanes), 0) == 0
    last_row = lax.broadcasted_iota(jnp.int32, (8, lanes), 0) == 7

    def plane(src, dst, k, above, below, forced):
        for i in range(strips):
            at = pl.ds(i * 8, 8)
            before = pl.ds((i - 1) % strips * 8, 8)
            after = pl.ds((i + 1) % strips * 8, 8)
            c_w = cw[k, at, :]
            c_e = ce[k, at, :]
            c_s = cs[k, at, :]
            c_n = cn[k, at, :]
            c_c = cc[k, at, :]
            c_8 = m8[at, :]
            for t in range(nt):
                p = t * nk + k
                cur = buf[src, p, at, :]
                south = jnp.where(first_row, pltpu.roll(buf[src, p, before, :], 1, 0), pltpu.roll(cur, 1, 0))
                north = jnp.where(last_row, pltpu.roll(buf[src, p, after, :], 7, 0), pltpu.roll(cur, 7, 0))
                west = pltpu.roll(cur, 1, 1)
                east = pltpu.roll(cur, lanes - 1, 1)
                up = cur if above is None else buf[src, t * nk + above, at, :]
                down = cur if below is None else buf[src, t * nk + below, at, :]
                tend = c_w * west + c_e * east + c_s * south + c_n * north + c_c * cur
                tend = tend + c_8 * (up + down)
                if forced:
                    tend = tend + mf[t, at, :]
                buf[dst, p, at, :] = cur + tend

    def step(i, carry):
        for src in (0, 1):
            dst = 1 - src
            for k in range(nk):
                plane(src, dst, k, k - 1 if k > 0 else None, k + 1 if k < nk - 1 else None, k == 0)
        return carry

    lax.fori_loop(0, STEPS // 2, step, 0)

    def out(p, carry):
        o_ref[p // nk, p % nk] = buf[STEPS % 2, p, :orows, :ocols]
        return carry

    lax.fori_loop(0, planes, out, 0)


def evolve(tracers, u_vel, v_vel, land_mask, forcing, halo, f_halo):
    nt, nk, orows, ocols = tracers.shape
    plane = (orows + 2 * WIDE, LANES)
    vm = lambda *shape: pltpu.VMEM(shape, jnp.float32)
    return pl.pallas_call(
        stencil_kernel,
        out_shape=jax.ShapeDtypeStruct(tracers.shape, jnp.float32),
        scratch_shapes=[
            vm(2, nt * nk, *plane),
            vm(nk, *plane),
            vm(nk, *plane),
            vm(*plane),
            vm(nt, *plane),
            vm(nk, *plane),
            vm(nk, *plane),
            vm(nk, *plane),
            vm(nk, *plane),
            vm(nk, *plane),
            vm(*plane),
            vm(nt, *plane),
        ],
        compiler_params=pltpu.CompilerParams(vmem_limit_bytes=62 * 1024 * 1024),
    )(tracers, u_vel, v_vel, land_mask, forcing, *halo, *f_halo)


def atmosphere_block(atm_flux):
    cols_n = lax.axis_size("ox")
    rows_n = lax.axis_size("oy")
    width = atm_flux.shape[2] // cols_n
    nf, lat = atm_flux.shape[:2]
    body = jnp.roll(atm_flux, H, axis=2).reshape(nf, lat, cols_n, width)
    tail = jnp.roll(atm_flux, H - width, axis=2).reshape(nf, lat, cols_n, width)[..., : 2 * H]
    pieces = jnp.concatenate([body, tail], axis=3)
    got = lax.all_to_all(pieces, "ox", split_axis=2, concat_axis=1, tiled=True)
    own = got.reshape(nf, -1, width + 2 * H)
    below = lax.ppermute(own[:, -H:], "oy", [(i, i + 1) for i in range(rows_n - 1)])
    above = lax.ppermute(own[:, :H], "oy", [(i + 1, i) for i in range(rows_n - 1)])
    return jnp.concatenate([below, own, above], axis=1)


def remap(padded, remap_index, remap_weight):
    nf, arows, acols = padded.shape
    kk, orows, ocols = remap_index.shape
    base_r = jnp.arange(orows, dtype=jnp.int32) * (arows - 2 * H - 1) // (orows - 1) + H
    base_c = jnp.arange(ocols, dtype=jnp.int32) * (acols - 2 * H - 1) // (ocols - 1) + H
    offs = jnp.arange(2 * H + 1, dtype=jnp.int32) - H
    pick_r = (
        (base_r[None, :, None] + offs[:, None, None])
        == jnp.arange(arows, dtype=jnp.int32)[None, None, :]
    ).astype(jnp.float32).reshape(-1, arows)
    pick_c = (
        jnp.arange(acols, dtype=jnp.int32)[:, None, None]
        == (base_c[None, None, :] + offs[None, :, None])
    ).astype(jnp.float32).reshape(acols, -1)
    lifted = jnp.einsum("pa,fab->fpb", pick_r, padded, precision=HIGH)
    window = jnp.einsum("fpb,bq->fpq", lifted, pick_c, precision=HIGH)
    window = window.reshape(nf, 2 * H + 1, orows, 2 * H + 1, ocols)
    row_of = remap_index // acols - base_r[None, :, None] + H
    col_of = remap_index % acols - base_c[None, None, :] + H
    inside = (row_of >= 0) & (row_of <= 2 * H) & (col_of >= 0) & (col_of <= 2 * H)
    slot = jnp.where(inside, row_of * (2 * H + 1) + col_of, -1)
    slots = jnp.arange((2 * H + 1) ** 2, dtype=jnp.int32)
    wsum = jnp.sum(
        jnp.where(slot[:, None] == slots[None, :, None, None], remap_weight[:, None], 0.0),
        axis=0,
    ).reshape(2 * H + 1, 2 * H + 1, orows, ocols)
    fast = jnp.sum(window * wsum.transpose(0, 2, 1, 3)[None], axis=(1, 3))
    missed = jnp.logical_not(jnp.all(inside))

    def general():
        flat = padded.reshape(nf, -1)
        total = jnp.zeros((nf,) + remap_index.shape[1:], jnp.float32)
        for source in range(kk):
            picked = jnp.take(flat, remap_index[source], axis=1)
            total = total + remap_weight[source][None] * picked
        return total

    return lax.cond(missed, general, lambda: fast)


def on_device(atm_flux, remap_index, remap_weight, coupling, land_mask, tracers, u_vel, v_vel):
    fields = [
        tracers.reshape((-1,) + tracers.shape[2:]),
        u_vel.astype(jnp.float32),
        v_vel.astype(jnp.float32),
        land_mask.astype(jnp.float32)[None],
    ]
    halo = exchange(fields, [False, True, True, False])

    padded = atmosphere_block(atm_flux)
    halo, padded = lax.optimization_barrier((halo, padded))
    ocean_flux = remap(padded, remap_index, remap_weight)
    forcing = jnp.sum(coupling[:, :, None, None] * ocean_flux[None], axis=1)
    sides, forcing = lax.optimization_barrier((halo[2], forcing))
    halo = (halo[0], halo[1], lane_tile(sides, tracers.shape[-1]))
    f_halo = exchange([forcing], [False])
    f_halo = (f_halo[0], f_halo[1], lane_tile(f_halo[2], tracers.shape[-1]))
    final = evolve(tracers, u_vel, v_vel, land_mask, forcing, halo, f_halo)
    return (ocean_flux, final)


def solution(mesh):
    placed = (
        P(None, ("oy", "ox"), None),
        P(None, "oy", "ox"),
        P(None, "oy", "ox"),
        P(),
        P("oy", "ox"),
        P(None, None, "oy", "ox"),
        P(None, "oy", "ox"),
        P(None, "oy", "ox"),
    )
    return jax.shard_map(
        on_device,
        mesh=mesh,
        in_specs=placed,
        out_specs=(P(None, "oy", "ox"), P(None, None, "oy", "ox")),
        check_vma=False,
    )
```

```python
import jax
import jax.numpy as jnp
from jax import lax
from jax.sharding import PartitionSpec as P
from jax.experimental import pallas as pl
from jax.experimental.pallas import tpu as pltpu

H = 2
STEPS = 8
WIDE = 8
LANES = 384
HIGH = lax.Precision.HIGHEST


def with_halo(cells, sides, width, closed):
    for axis, dim in sides:
        count = lax.axis_size(axis)
        ends = count if closed else count - 1
        head = lax.slice_in_dim(cells, 0, width, axis=dim)
        tail = lax.slice_in_dim(cells, cells.shape[dim] - width, cells.shape[dim], axis=dim)
        cells = jnp.concatenate(
            [
                lax.ppermute(tail, axis, [(i, (i + 1) % count) for i in range(ends)]),
                cells,
                lax.ppermute(head, axis, [((i + 1) % count, i) for i in range(ends)]),
            ],
            axis=dim,
        )
    return cells


def exchange(blocks, flips):
    rows_n = lax.axis_size("oy")
    cols_n = lax.axis_size("ox")
    on_top = lax.axis_index("oy") == rows_n - 1
    sizes = [b.shape[0] for b in blocks]
    sign = jnp.concatenate(
        [jnp.full((n,), -1.0 if neg else 1.0, jnp.float32) for n, neg in zip(sizes, flips)]
    )[:, None, None]
    tops = jnp.concatenate([b[:, -WIDE:, :] for b in blocks], axis=0)
    bots = jnp.concatenate([b[:, :WIDE, :] for b in blocks], axis=0)
    south = lax.ppermute(tops, "oy", [(i, i + 1) for i in range(rows_n - 1)])
    north = lax.ppermute(bots, "oy", [(i + 1, i) for i in range(rows_n - 1)])
    top_row = (rows_n - 1) * cols_n
    fold = lax.ppermute(
        tops,
        ("oy", "ox"),
        [(top_row + (cols_n // 2 - j) % cols_n, top_row + j) for j in range(cols_n)],
    )
    north = jnp.where(on_top, fold[:, ::-1, ::-1] * sign, north)
    easts = jnp.concatenate(
        [jnp.concatenate([b[..., -WIDE:] for b in blocks], axis=0), north[..., -WIDE:], south[..., -WIDE:]],
        axis=1,
    )
    wests = jnp.concatenate(
        [jnp.concatenate([b[..., :WIDE] for b in blocks], axis=0), north[..., :WIDE], south[..., :WIDE]],
        axis=1,
    )
    from_w = lax.ppermute(easts, "ox", [(i, (i + 1) % cols_n) for i in range(cols_n)])
    from_e = lax.ppermute(wests, "ox", [((i + 1) % cols_n, i) for i in range(cols_n)])
    return north, south, (from_e, from_w)


def lane_tile(sides, cols):
    from_e, from_w = sides
    gap = jnp.zeros(from_e.shape[:-1] + (LANES - cols - 2 * WIDE,), jnp.float32)
    return jnp.concatenate([from_e, gap, from_w], axis=-1)


def stencil_kernel(tr_ref, u_ref, v_ref, m_ref, f_ref, hn_ref, hs_ref, hc_ref, fn_ref, fs_ref, fc_ref,
                   o_ref, buf, uu, vv, mm, ff, cw, ce, cs, cn, cc, m8, mf):
    nt, nk, orows, ocols = tr_ref.shape
    _, planes, rows, lanes = buf.shape

    def place(dst, own, at):
        dst[:orows, :ocols] = own
        dst[orows:orows + WIDE, :ocols] = hn_ref[at]
        dst[orows + WIDE:, :ocols] = hs_ref[at]
        dst[:, ocols:] = hc_ref[at]

    def fill(p, carry):
        place(buf.at[0, p], tr_ref[p // nk, p % nk], p)
        return carry

    lax.fori_loop(0, planes, fill, 0)

    def fill_uv(k, carry):
        place(uu.at[k], u_ref[k].astype(jnp.float32), planes + k)
        place(vv.at[k], v_ref[k].astype(jnp.float32), planes + nk + k)
        return carry

    lax.fori_loop(0, nk, fill_uv, 0)
    place(mm, m_ref[...].astype(jnp.float32), planes + 2 * nk)
    for t in range(nt):
        ff[t, :orows, :ocols] = f_ref[t]
        ff[t, orows:orows + WIDE, :ocols] = fn_ref[t]
        ff[t, orows + WIDE:, :ocols] = fs_ref[t]
        ff[t, :, ocols:] = fc_ref[t]

    mask = mm[...]
    m8[...] = mask * 0.08
    for t in range(nt):
        mf[t] = mask * ff[t]

    def coef(k, carry):
        u = uu[k]
        v = vv[k]
        up = jnp.maximum(u, 0.0)
        um = jnp.minimum(u, 0.0)
        vp = jnp.maximum(v, 0.0)
        vm = jnp.minimum(v, 0.0)
        cw[k] = mask * (up + 0.08)
        ce[k] = mask * (0.08 - um)
        cs[k] = mask * (vp + 0.08)
        cn[k] = mask * (0.08 - vm)
        cc[k] = mask * ((um - up) + (vm - vp) - 0.48)
        return carry

    lax.fori_loop(0, nk, coef, 0)

    strips = rows // 8
    first_row = lax.broadcasted_iota(jnp.int32, (8, lanes), 0) == 0
    last_row = lax.broadcasted_iota(jnp.int32, (8, lanes), 0) == 7

    def plane(src, dst, k, above, below, forced):
        for i in range(strips):
            at = pl.ds(i * 8, 8)
            before = pl.ds((i - 1) % strips * 8, 8)
            after = pl.ds((i + 1) % strips * 8, 8)
            c_w = cw[k, at, :]
            c_e = ce[k, at, :]
            c_s = cs[k, at, :]
            c_n = cn[k, at, :]
            c_c = cc[k, at, :]
            c_8 = m8[at, :]
            for t in range(nt):
                p = t * nk + k
                cur = buf[src, p, at, :]
                south = jnp.where(first_row, pltpu.roll(buf[src, p, before, :], 1, 0), pltpu.roll(cur, 1, 0))
                north = jnp.where(last_row, pltpu.roll(buf[src, p, after, :], 7, 0), pltpu.roll(cur, 7, 0))
                west = pltpu.roll(cur, 1, 1)
                east = pltpu.roll(cur, lanes - 1, 1)
                up = cur if above is None else buf[src, t * nk + above, at, :]
                down = cur if below is None else buf[src, t * nk + below, at, :]
                tend = c_w * west + c_e * east + c_s * south + c_n * north + c_c * cur
                tend = tend + c_8 * (up + down)
                if forced:
                    tend = tend + mf[t, at, :]
                buf[dst, p, at, :] = cur + tend

    def step(i, carry):
        for src in (0, 1):
            dst = 1 - src
            for k in range(nk):
                plane(src, dst, k, k - 1 if k > 0 else None, k + 1 if k < nk - 1 else None, k == 0)
        return carry

    lax.fori_loop(0, STEPS // 2, step, 0)

    def out(p, carry):
        o_ref[p // nk, p % nk] = buf[STEPS % 2, p, :orows, :ocols]
        return carry

    lax.fori_loop(0, planes, out, 0)


def evolve(tracers, u_vel, v_vel, land_mask, forcing, halo, f_halo):
    nt, nk, orows, ocols = tracers.shape
    plane = (orows + 2 * WIDE, LANES)
    vm = lambda *shape: pltpu.VMEM(shape, jnp.float32)
    return pl.pallas_call(
        stencil_kernel,
        out_shape=jax.ShapeDtypeStruct(tracers.shape, jnp.float32),
        scratch_shapes=[
            vm(2, nt * nk, *plane),
            vm(nk, *plane),
            vm(nk, *plane),
            vm(*plane),
            vm(nt, *plane),
            vm(nk, *plane),
            vm(nk, *plane),
            vm(nk, *plane),
            vm(nk, *plane),
            vm(nk, *plane),
            vm(*plane),
            vm(nt, *plane),
        ],
        compiler_params=pltpu.CompilerParams(vmem_limit_bytes=62 * 1024 * 1024),
    )(tracers, u_vel, v_vel, land_mask, forcing, *halo, *f_halo)


def atmosphere_block(atm_flux):
    cols_n = lax.axis_size("ox")
    rows_n = lax.axis_size("oy")
    width = atm_flux.shape[2] // cols_n
    nf, lat = atm_flux.shape[:2]
    body = jnp.roll(atm_flux, H, axis=2).reshape(nf, lat, cols_n, width)
    tail = jnp.roll(atm_flux, H - width, axis=2).reshape(nf, lat, cols_n, width)[..., : 2 * H]
    pieces = jnp.concatenate([body, tail], axis=3)
    got = lax.all_to_all(pieces, "ox", split_axis=2, concat_axis=1, tiled=True)
    own = got.reshape(nf, -1, width + 2 * H)
    below = lax.ppermute(own[:, -H:], "oy", [(i, i + 1) for i in range(rows_n - 1)])
    above = lax.ppermute(own[:, :H], "oy", [(i + 1, i) for i in range(rows_n - 1)])
    return jnp.concatenate([below, own, above], axis=1)


def remap(padded, remap_index, remap_weight):
    nf, arows, acols = padded.shape
    kk, orows, ocols = remap_index.shape
    base_r = jnp.arange(orows, dtype=jnp.int32) * (arows - 2 * H - 1) // (orows - 1) + H
    base_c = jnp.arange(ocols, dtype=jnp.int32) * (acols - 2 * H - 1) // (ocols - 1) + H
    offs = jnp.arange(2 * H + 1, dtype=jnp.int32) - H
    pick_c = (
        jnp.arange(acols, dtype=jnp.int32)[:, None, None]
        == (base_c[None, None, :] + offs[None, :, None])
    ).astype(jnp.float32).reshape(acols, -1)
    lifted = jnp.einsum("fab,bq->faq", padded, pick_c, precision=HIGH)
    lifted = lifted.reshape(nf, arows, 2 * H + 1, ocols)
    window = lifted[:, base_r[None, :] + offs[:, None]]
    row_of = remap_index // acols - base_r[None, :, None] + H
    col_of = remap_index % acols - base_c[None, None, :] + H
    inside = (row_of >= 0) & (row_of <= 2 * H) & (col_of >= 0) & (col_of <= 2 * H)
    slot = jnp.where(inside, row_of * (2 * H + 1) + col_of, -1)
    slots = jnp.arange((2 * H + 1) ** 2, dtype=jnp.int32)
    wsum = jnp.sum(
        jnp.where(slot[:, None] == slots[None, :, None, None], remap_weight[:, None], 0.0),
        axis=0,
    ).reshape(2 * H + 1, 2 * H + 1, orows, ocols)
    fast = jnp.sum(window * wsum.transpose(0, 2, 1, 3)[None], axis=(1, 3))
    missed = jnp.logical_not(jnp.all(inside))

    def general():
        flat = padded.reshape(nf, -1)
        total = jnp.zeros((nf,) + remap_index.shape[1:], jnp.float32)
        for source in range(kk):
            picked = jnp.take(flat, remap_index[source], axis=1)
            total = total + remap_weight[source][None] * picked
        return total

    return lax.cond(missed, general, lambda: fast)


def on_device(atm_flux, remap_index, remap_weight, coupling, land_mask, tracers, u_vel, v_vel):
    fields = [
        tracers.reshape((-1,) + tracers.shape[2:]),
        u_vel.astype(jnp.float32),
        v_vel.astype(jnp.float32),
        land_mask.astype(jnp.float32)[None],
    ]
    halo = exchange(fields, [False, True, True, False])

    padded = atmosphere_block(atm_flux)
    halo, padded = lax.optimization_barrier((halo, padded))
    ocean_flux = remap(padded, remap_index, remap_weight)
    forcing = jnp.sum(coupling[:, :, None, None] * ocean_flux[None], axis=1)
    sides, forcing = lax.optimization_barrier((halo[2], forcing))
    halo = (halo[0], halo[1], lane_tile(sides, tracers.shape[-1]))
    f_halo = exchange([forcing], [False])
    f_halo = (f_halo[0], f_halo[1], lane_tile(f_halo[2], tracers.shape[-1]))
    final = evolve(tracers, u_vel, v_vel, land_mask, forcing, halo, f_halo)
    return (ocean_flux, final)


def solution(mesh):
    placed = (
        P(None, ("oy", "ox"), None),
        P(None, "oy", "ox"),
        P(None, "oy", "ox"),
        P(),
        P("oy", "ox"),
        P(None, None, "oy", "ox"),
        P(None, "oy", "ox"),
        P(None, "oy", "ox"),
    )
    return jax.shard_map(
        on_device,
        mesh=mesh,
        in_specs=placed,
        out_specs=(P(None, "oy", "ox"), P(None, None, "oy", "ox")),
        check_vma=False,
    )
```

```python
import jax
import jax.numpy as jnp
from jax import lax
from jax.sharding import PartitionSpec as P
from jax.experimental import pallas as pl
from jax.experimental.pallas import tpu as pltpu

H = 2
STEPS = 8
WIDE = 8
LANES = 384
HIGH = lax.Precision.HIGHEST


def with_halo(cells, sides, width, closed):
    for axis, dim in sides:
        count = lax.axis_size(axis)
        ends = count if closed else count - 1
        head = lax.slice_in_dim(cells, 0, width, axis=dim)
        tail = lax.slice_in_dim(cells, cells.shape[dim] - width, cells.shape[dim], axis=dim)
        cells = jnp.concatenate(
            [
                lax.ppermute(tail, axis, [(i, (i + 1) % count) for i in range(ends)]),
                cells,
                lax.ppermute(head, axis, [((i + 1) % count, i) for i in range(ends)]),
            ],
            axis=dim,
        )
    return cells


def exchange(blocks, flips):
    rows_n = lax.axis_size("oy")
    cols_n = lax.axis_size("ox")
    on_top = lax.axis_index("oy") == rows_n - 1
    sizes = [b.shape[0] for b in blocks]
    sign = jnp.concatenate(
        [jnp.full((n,), -1.0 if neg else 1.0, jnp.float32) for n, neg in zip(sizes, flips)]
    )[:, None, None]
    tops = jnp.concatenate([b[:, -WIDE:, :] for b in blocks], axis=0)
    bots = jnp.concatenate([b[:, :WIDE, :] for b in blocks], axis=0)
    south = lax.ppermute(tops, "oy", [(i, i + 1) for i in range(rows_n - 1)])
    north = lax.ppermute(bots, "oy", [(i + 1, i) for i in range(rows_n - 1)])
    top_row = (rows_n - 1) * cols_n
    fold = lax.ppermute(
        tops,
        ("oy", "ox"),
        [(top_row + (cols_n // 2 - j) % cols_n, top_row + j) for j in range(cols_n)],
    )
    north = jnp.where(on_top, fold[:, ::-1, ::-1] * sign, north)
    easts = jnp.concatenate(
        [jnp.concatenate([b[..., -WIDE:] for b in blocks], axis=0), north[..., -WIDE:], south[..., -WIDE:]],
        axis=1,
    )
    wests = jnp.concatenate(
        [jnp.concatenate([b[..., :WIDE] for b in blocks], axis=0), north[..., :WIDE], south[..., :WIDE]],
        axis=1,
    )
    from_w = lax.ppermute(easts, "ox", [(i, (i + 1) % cols_n) for i in range(cols_n)])
    from_e = lax.ppermute(wests, "ox", [((i + 1) % cols_n, i) for i in range(cols_n)])
    return north, south, (from_e, from_w)


def lane_tile(sides, cols):
    from_e, from_w = sides
    gap = jnp.zeros(from_e.shape[:-1] + (LANES - cols - 2 * WIDE,), jnp.float32)
    return jnp.concatenate([from_e, gap, from_w], axis=-1)


def stencil_kernel(tr_ref, u_ref, v_ref, m_ref, f_ref, hn_ref, hs_ref, hc_ref, fn_ref, fs_ref, fc_ref,
                   o_ref, buf, uu, vv, mm, ff, cw, ce, cs, cn, cc, m8, mf):
    nt, nk, orows, ocols = tr_ref.shape
    _, planes, rows, lanes = buf.shape

    def place(dst, own, at):
        dst[:orows, :ocols] = own
        dst[orows:orows + WIDE, :ocols] = hn_ref[at]
        dst[orows + WIDE:, :ocols] = hs_ref[at]
        dst[:, ocols:] = hc_ref[at]

    def fill(p, carry):
        place(buf.at[0, p], tr_ref[p // nk, p % nk], p)
        return carry

    lax.fori_loop(0, planes, fill, 0)

    def fill_uv(k, carry):
        place(uu.at[k], u_ref[k].astype(jnp.float32), planes + k)
        place(vv.at[k], v_ref[k].astype(jnp.float32), planes + nk + k)
        return carry

    lax.fori_loop(0, nk, fill_uv, 0)
    place(mm, m_ref[...].astype(jnp.float32), planes + 2 * nk)
    for t in range(nt):
        ff[t, :orows, :ocols] = f_ref[t]
        ff[t, orows:orows + WIDE, :ocols] = fn_ref[t]
        ff[t, orows + WIDE:, :ocols] = fs_ref[t]
        ff[t, :, ocols:] = fc_ref[t]

    mask = mm[...]
    m8[...] = mask * 0.08
    for t in range(nt):
        mf[t] = mask * ff[t]

    def coef(k, carry):
        u = uu[k]
        v = vv[k]
        up = jnp.maximum(u, 0.0)
        um = jnp.minimum(u, 0.0)
        vp = jnp.maximum(v, 0.0)
        vm = jnp.minimum(v, 0.0)
        cw[k] = mask * (up + 0.08)
        ce[k] = mask * (0.08 - um)
        cs[k] = mask * (vp + 0.08)
        cn[k] = mask * (0.08 - vm)
        cc[k] = 1.0 + mask * ((um - up) + (vm - vp) - 0.48)
        return carry

    lax.fori_loop(0, nk, coef, 0)

    strips = rows // 8
    first_row = lax.broadcasted_iota(jnp.int32, (8, lanes), 0) == 0
    last_row = lax.broadcasted_iota(jnp.int32, (8, lanes), 0) == 7

    def plane(src, dst, k, above, below, forced):
        for i in range(strips):
            at = pl.ds(i * 8, 8)
            before = pl.ds((i - 1) % strips * 8, 8)
            after = pl.ds((i + 1) % strips * 8, 8)
            c_w = cw[k, at, :]
            c_e = ce[k, at, :]
            c_s = cs[k, at, :]
            c_n = cn[k, at, :]
            c_c = cc[k, at, :]
            c_8 = m8[at, :]
            for t in range(nt):
                p = t * nk + k
                cur = buf[src, p, at, :]
                south = jnp.where(first_row, pltpu.roll(buf[src, p, before, :], 1, 0), pltpu.roll(cur, 1, 0))
                north = jnp.where(last_row, pltpu.roll(buf[src, p, after, :], 7, 0), pltpu.roll(cur, 7, 0))
                west = pltpu.roll(cur, 1, 1)
                east = pltpu.roll(cur, lanes - 1, 1)
                up = cur if above is None else buf[src, t * nk + above, at, :]
                down = cur if below is None else buf[src, t * nk + below, at, :]
                new = c_w * west + c_e * east + c_s * south + c_n * north + c_c * cur
                new = new + c_8 * (up + down)
                if forced:
                    new = new + mf[t, at, :]
                buf[dst, p, at, :] = new

    def step(i, carry):
        for src in (0, 1):
            dst = 1 - src
            for k in range(nk):
                plane(src, dst, k, k - 1 if k > 0 else None, k + 1 if k < nk - 1 else None, k == 0)
        return carry

    lax.fori_loop(0, STEPS // 2, step, 0)

    def out(p, carry):
        o_ref[p // nk, p % nk] = buf[STEPS % 2, p, :orows, :ocols]
        return carry

    lax.fori_loop(0, planes, out, 0)


def evolve(tracers, u_vel, v_vel, land_mask, forcing, halo, f_halo):
    nt, nk, orows, ocols = tracers.shape
    plane = (orows + 2 * WIDE, LANES)
    vm = lambda *shape: pltpu.VMEM(shape, jnp.float32)
    return pl.pallas_call(
        stencil_kernel,
        out_shape=jax.ShapeDtypeStruct(tracers.shape, jnp.float32),
        scratch_shapes=[
            vm(2, nt * nk, *plane),
            vm(nk, *plane),
            vm(nk, *plane),
            vm(*plane),
            vm(nt, *plane),
            vm(nk, *plane),
            vm(nk, *plane),
            vm(nk, *plane),
            vm(nk, *plane),
            vm(nk, *plane),
            vm(*plane),
            vm(nt, *plane),
        ],
        compiler_params=pltpu.CompilerParams(vmem_limit_bytes=62 * 1024 * 1024),
    )(tracers, u_vel, v_vel, land_mask, forcing, *halo, *f_halo)


def atmosphere_block(atm_flux):
    cols_n = lax.axis_size("ox")
    rows_n = lax.axis_size("oy")
    width = atm_flux.shape[2] // cols_n
    nf, lat = atm_flux.shape[:2]
    body = jnp.roll(atm_flux, H, axis=2).reshape(nf, lat, cols_n, width)
    tail = jnp.roll(atm_flux, H - width, axis=2).reshape(nf, lat, cols_n, width)[..., : 2 * H]
    pieces = jnp.concatenate([body, tail], axis=3)
    got = lax.all_to_all(pieces, "ox", split_axis=2, concat_axis=1, tiled=True)
    own = got.reshape(nf, -1, width + 2 * H)
    below = lax.ppermute(own[:, -H:], "oy", [(i, i + 1) for i in range(rows_n - 1)])
    above = lax.ppermute(own[:, :H], "oy", [(i + 1, i) for i in range(rows_n - 1)])
    return jnp.concatenate([below, own, above], axis=1)


def remap(padded, remap_index, remap_weight):
    nf, arows, acols = padded.shape
    kk, orows, ocols = remap_index.shape
    base_r = jnp.arange(orows, dtype=jnp.int32) * (arows - 2 * H - 1) // (orows - 1) + H
    base_c = jnp.arange(ocols, dtype=jnp.int32) * (acols - 2 * H - 1) // (ocols - 1) + H
    offs = jnp.arange(2 * H + 1, dtype=jnp.int32) - H
    pick_c = (
        jnp.arange(acols, dtype=jnp.int32)[:, None, None]
        == (base_c[None, None, :] + offs[None, :, None])
    ).astype(jnp.float32).reshape(acols, -1)
    lifted = jnp.einsum("fab,bq->faq", padded, pick_c, precision=HIGH)
    lifted = lifted.reshape(nf, arows, 2 * H + 1, ocols)
    window = lifted[:, base_r[None, :] + offs[:, None]]
    row_of = remap_index // acols - base_r[None, :, None] + H
    col_of = remap_index % acols - base_c[None, None, :] + H
    inside = (row_of >= 0) & (row_of <= 2 * H) & (col_of >= 0) & (col_of <= 2 * H)
    ar = jnp.arange(2 * H + 1, dtype=jnp.int32)
    hit = (row_of[:, None, :, None, :] == ar[None, :, None, None, None]) & (
        col_of[:, None, :, None, :] == ar[None, None, None, :, None]
    )
    wsum = jnp.sum(jnp.where(hit, remap_weight[:, None, :, None, :], 0.0), axis=0)
    fast = jnp.sum(window * wsum[None], axis=(1, 3))
    missed = jnp.logical_not(jnp.all(inside))

    def general():
        flat = padded.reshape(nf, -1)
        total = jnp.zeros((nf,) + remap_index.shape[1:], jnp.float32)
        for source in range(kk):
            picked = jnp.take(flat, remap_index[source], axis=1)
            total = total + remap_weight[source][None] * picked
        return total

    return lax.cond(missed, general, lambda: fast)


def on_device(atm_flux, remap_index, remap_weight, coupling, land_mask, tracers, u_vel, v_vel):
    fields = [
        tracers.reshape((-1,) + tracers.shape[2:]),
        u_vel.astype(jnp.float32),
        v_vel.astype(jnp.float32),
        land_mask.astype(jnp.float32)[None],
    ]
    halo = exchange(fields, [False, True, True, False])

    padded = atmosphere_block(atm_flux)
    halo, padded = lax.optimization_barrier((halo, padded))
    ocean_flux = remap(padded, remap_index, remap_weight)
    forcing = jnp.sum(coupling[:, :, None, None] * ocean_flux[None], axis=1)
    sides, forcing = lax.optimization_barrier((halo[2], forcing))
    halo = (halo[0], halo[1], lane_tile(sides, tracers.shape[-1]))
    f_halo = exchange([forcing], [False])
    f_halo = (f_halo[0], f_halo[1], lane_tile(f_halo[2], tracers.shape[-1]))
    final = evolve(tracers, u_vel, v_vel, land_mask, forcing, halo, f_halo)
    return (ocean_flux, final)


def solution(mesh):
    placed = (
        P(None, ("oy", "ox"), None),
        P(None, "oy", "ox"),
        P(None, "oy", "ox"),
        P(),
        P("oy", "ox"),
        P(None, None, "oy", "ox"),
        P(None, "oy", "ox"),
        P(None, "oy", "ox"),
    )
    return jax.shard_map(
        on_device,
        mesh=mesh,
        in_specs=placed,
        out_specs=(P(None, "oy", "ox"), P(None, None, "oy", "ox")),
        check_vma=False,
    )
```

```python
import jax
import jax.numpy as jnp
from jax import lax
from jax.sharding import PartitionSpec as P
from jax.experimental import pallas as pl
from jax.experimental.pallas import tpu as pltpu

H = 2
STEPS = 8
WIDE = 8
LANES = 384
HIGH = lax.Precision.HIGHEST


def with_halo(cells, sides, width, closed):
    for axis, dim in sides:
        count = lax.axis_size(axis)
        ends = count if closed else count - 1
        head = lax.slice_in_dim(cells, 0, width, axis=dim)
        tail = lax.slice_in_dim(cells, cells.shape[dim] - width, cells.shape[dim], axis=dim)
        cells = jnp.concatenate(
            [
                lax.ppermute(tail, axis, [(i, (i + 1) % count) for i in range(ends)]),
                cells,
                lax.ppermute(head, axis, [((i + 1) % count, i) for i in range(ends)]),
            ],
            axis=dim,
        )
    return cells


def exchange(blocks, flips):
    rows_n = lax.axis_size("oy")
    cols_n = lax.axis_size("ox")
    on_top = lax.axis_index("oy") == rows_n - 1
    sizes = [b.shape[0] for b in blocks]
    sign = jnp.concatenate(
        [jnp.full((n,), -1.0 if neg else 1.0, jnp.float32) for n, neg in zip(sizes, flips)]
    )[:, None, None]
    tops = jnp.concatenate([b[:, -WIDE:, :] for b in blocks], axis=0)
    bots = jnp.concatenate([b[:, :WIDE, :] for b in blocks], axis=0)
    south = lax.ppermute(tops, "oy", [(i, i + 1) for i in range(rows_n - 1)])
    north = lax.ppermute(bots, "oy", [(i + 1, i) for i in range(rows_n - 1)])
    top_row = (rows_n - 1) * cols_n
    fold = lax.ppermute(
        tops,
        ("oy", "ox"),
        [(top_row + (cols_n // 2 - j) % cols_n, top_row + j) for j in range(cols_n)],
    )
    north = jnp.where(on_top, fold[:, ::-1, ::-1] * sign, north)
    easts = jnp.concatenate(
        [jnp.concatenate([b[..., -WIDE:] for b in blocks], axis=0), north[..., -WIDE:], south[..., -WIDE:]],
        axis=1,
    )
    wests = jnp.concatenate(
        [jnp.concatenate([b[..., :WIDE] for b in blocks], axis=0), north[..., :WIDE], south[..., :WIDE]],
        axis=1,
    )
    from_w = lax.ppermute(easts.swapaxes(1, 2), "ox", [(i, (i + 1) % cols_n) for i in range(cols_n)])
    from_e = lax.ppermute(wests.swapaxes(1, 2), "ox", [((i + 1) % cols_n, i) for i in range(cols_n)])
    return north, south, (from_e.swapaxes(1, 2), from_w.swapaxes(1, 2))


def lane_tile(sides, cols):
    from_e, from_w = sides
    gap = jnp.zeros(from_e.shape[:-1] + (LANES - cols - 2 * WIDE,), jnp.float32)
    return jnp.concatenate([from_e, gap, from_w], axis=-1)


def stencil_kernel(tr_ref, u_ref, v_ref, m_ref, f_ref, hn_ref, hs_ref, hc_ref, fn_ref, fs_ref, fc_ref,
                   o_ref, buf, uu, vv, mm, ff, cw, ce, cs, cn, cc, m8, mf):
    nt, nk, orows, ocols = tr_ref.shape
    _, planes, rows, lanes = buf.shape

    def place(dst, own, at):
        dst[:orows, :ocols] = own
        dst[orows:orows + WIDE, :ocols] = hn_ref[at]
        dst[orows + WIDE:, :ocols] = hs_ref[at]
        dst[:, ocols:] = hc_ref[at]

    def fill(p, carry):
        place(buf.at[0, p], tr_ref[p // nk, p % nk], p)
        return carry

    lax.fori_loop(0, planes, fill, 0)

    def fill_uv(k, carry):
        place(uu.at[k], u_ref[k].astype(jnp.float32), planes + k)
        place(vv.at[k], v_ref[k].astype(jnp.float32), planes + nk + k)
        return carry

    lax.fori_loop(0, nk, fill_uv, 0)
    place(mm, m_ref[...].astype(jnp.float32), planes + 2 * nk)
    for t in range(nt):
        ff[t, :orows, :ocols] = f_ref[t]
        ff[t, orows:orows + WIDE, :ocols] = fn_ref[t]
        ff[t, orows + WIDE:, :ocols] = fs_ref[t]
        ff[t, :, ocols:] = fc_ref[t]

    mask = mm[...]
    m8[...] = mask * 0.08
    for t in range(nt):
        mf[t] = mask * ff[t]

    def coef(k, carry):
        u = uu[k]
        v = vv[k]
        up = jnp.maximum(u, 0.0)
        um = jnp.minimum(u, 0.0)
        vp = jnp.maximum(v, 0.0)
        vm = jnp.minimum(v, 0.0)
        cw[k] = mask * (up + 0.08)
        ce[k] = mask * (0.08 - um)
        cs[k] = mask * (vp + 0.08)
        cn[k] = mask * (0.08 - vm)
        cc[k] = mask * ((um - up) + (vm - vp) - 0.48)
        return carry

    lax.fori_loop(0, nk, coef, 0)

    strips = rows // 8
    first_row = lax.broadcasted_iota(jnp.int32, (8, lanes), 0) == 0
    last_row = lax.broadcasted_iota(jnp.int32, (8, lanes), 0) == 7

    def plane(src, dst, k, above, below, forced):
        for i in range(strips):
            at = pl.ds(i * 8, 8)
            before = pl.ds((i - 1) % strips * 8, 8)
            after = pl.ds((i + 1) % strips * 8, 8)
            c_w = cw[k, at, :]
            c_e = ce[k, at, :]
            c_s = cs[k, at, :]
            c_n = cn[k, at, :]
            c_c = cc[k, at, :]
            c_8 = m8[at, :]
            for t in range(nt):
                p = t * nk + k
                cur = buf[src, p, at, :]
                south = jnp.where(first_row, pltpu.roll(buf[src, p, before, :], 1, 0), pltpu.roll(cur, 1, 0))
                north = jnp.where(last_row, pltpu.roll(buf[src, p, after, :], 7, 0), pltpu.roll(cur, 7, 0))
                west = pltpu.roll(cur, 1, 1)
                east = pltpu.roll(cur, lanes - 1, 1)
                up = cur if above is None else buf[src, t * nk + above, at, :]
                down = cur if below is None else buf[src, t * nk + below, at, :]
                tend = c_w * west + c_e * east + c_s * south + c_n * north + c_c * cur
                tend = tend + c_8 * (up + down)
                if forced:
                    tend = tend + mf[t, at, :]
                buf[dst, p, at, :] = cur + tend

    def step(i, carry):
        for src in (0, 1):
            dst = 1 - src
            for k in range(nk):
                plane(src, dst, k, k - 1 if k > 0 else None, k + 1 if k < nk - 1 else None, k == 0)
        return carry

    lax.fori_loop(0, STEPS // 2, step, 0)

    def out(p, carry):
        o_ref[p // nk, p % nk] = buf[STEPS % 2, p, :orows, :ocols]
        return carry

    lax.fori_loop(0, planes, out, 0)


def evolve(tracers, u_vel, v_vel, land_mask, forcing, halo, f_halo):
    nt, nk, orows, ocols = tracers.shape
    plane = (orows + 2 * WIDE, LANES)
    vm = lambda *shape: pltpu.VMEM(shape, jnp.float32)
    return pl.pallas_call(
        stencil_kernel,
        out_shape=jax.ShapeDtypeStruct(tracers.shape, jnp.float32),
        scratch_shapes=[
            vm(2, nt * nk, *plane),
            vm(nk, *plane),
            vm(nk, *plane),
            vm(*plane),
            vm(nt, *plane),
            vm(nk, *plane),
            vm(nk, *plane),
            vm(nk, *plane),
            vm(nk, *plane),
            vm(nk, *plane),
            vm(*plane),
            vm(nt, *plane),
        ],
        compiler_params=pltpu.CompilerParams(vmem_limit_bytes=62 * 1024 * 1024),
    )(tracers, u_vel, v_vel, land_mask, forcing, *halo, *f_halo)


def atmosphere_block(atm_flux):
    cols_n = lax.axis_size("ox")
    rows_n = lax.axis_size("oy")
    width = atm_flux.shape[2] // cols_n
    nf, lat = atm_flux.shape[:2]
    body = jnp.roll(atm_flux, H, axis=2).reshape(nf, lat, cols_n, width)
    tail = jnp.roll(atm_flux, H - width, axis=2).reshape(nf, lat, cols_n, width)[..., : 2 * H]
    pieces = jnp.concatenate([body, tail], axis=3)
    got = lax.all_to_all(pieces, "ox", split_axis=2, concat_axis=1, tiled=True)
    own = got.reshape(nf, -1, width + 2 * H)
    below = lax.ppermute(own[:, -H:], "oy", [(i, i + 1) for i in range(rows_n - 1)])
    above = lax.ppermute(own[:, :H], "oy", [(i + 1, i) for i in range(rows_n - 1)])
    return jnp.concatenate([below, own, above], axis=1)


def remap(padded, remap_index, remap_weight):
    nf, arows, acols = padded.shape
    kk, orows, ocols = remap_index.shape
    base_r = jnp.arange(orows, dtype=jnp.int32) * (arows - 2 * H - 1) // (orows - 1) + H
    base_c = jnp.arange(ocols, dtype=jnp.int32) * (acols - 2 * H - 1) // (ocols - 1) + H
    offs = jnp.arange(2 * H + 1, dtype=jnp.int32) - H
    pick_c = (
        jnp.arange(acols, dtype=jnp.int32)[:, None, None]
        == (base_c[None, None, :] + offs[None, :, None])
    ).astype(jnp.float32).reshape(acols, -1)
    lifted = jnp.einsum("fab,bq->faq", padded, pick_c, precision=HIGH)
    lifted = lifted.reshape(nf, arows, 2 * H + 1, ocols)
    window = lifted[:, base_r[None, :] + offs[:, None]]
    row_of = remap_index // acols - base_r[None, :, None] + H
    col_of = remap_index % acols - base_c[None, None, :] + H
    inside = (row_of >= 0) & (row_of <= 2 * H) & (col_of >= 0) & (col_of <= 2 * H)
    slot = jnp.where(inside, row_of * (2 * H + 1) + col_of, -1)
    slots = jnp.arange((2 * H + 1) ** 2, dtype=jnp.int32)
    wsum = jnp.sum(
        jnp.where(slot[:, None] == slots[None, :, None, None], remap_weight[:, None], 0.0),
        axis=0,
    ).reshape(2 * H + 1, 2 * H + 1, orows, ocols)
    fast = jnp.sum(window * wsum.transpose(0, 2, 1, 3)[None], axis=(1, 3))
    missed = jnp.logical_not(jnp.all(inside))

    def general():
        flat = padded.reshape(nf, -1)
        total = jnp.zeros((nf,) + remap_index.shape[1:], jnp.float32)
        for source in range(kk):
            picked = jnp.take(flat, remap_index[source], axis=1)
            total = total + remap_weight[source][None] * picked
        return total

    return lax.cond(missed, general, lambda: fast)


def on_device(atm_flux, remap_index, remap_weight, coupling, land_mask, tracers, u_vel, v_vel):
    fields = [
        tracers.reshape((-1,) + tracers.shape[2:]),
        u_vel.astype(jnp.float32),
        v_vel.astype(jnp.float32),
        land_mask.astype(jnp.float32)[None],
    ]
    halo = exchange(fields, [False, True, True, False])

    padded = atmosphere_block(atm_flux)
    halo, padded = lax.optimization_barrier((halo, padded))
    ocean_flux = remap(padded, remap_index, remap_weight)
    forcing = jnp.sum(coupling[:, :, None, None] * ocean_flux[None], axis=1)
    sides, forcing = lax.optimization_barrier((halo[2], forcing))
    halo = (halo[0], halo[1], lane_tile(sides, tracers.shape[-1]))
    f_halo = exchange([forcing], [False])
    f_halo = (f_halo[0], f_halo[1], lane_tile(f_halo[2], tracers.shape[-1]))
    final = evolve(tracers, u_vel, v_vel, land_mask, forcing, halo, f_halo)
    return (ocean_flux, final)


def solution(mesh):
    placed = (
        P(None, ("oy", "ox"), None),
        P(None, "oy", "ox"),
        P(None, "oy", "ox"),
        P(),
        P("oy", "ox"),
        P(None, None, "oy", "ox"),
        P(None, "oy", "ox"),
        P(None, "oy", "ox"),
    )
    return jax.shard_map(
        on_device,
        mesh=mesh,
        in_specs=placed,
        out_specs=(P(None, "oy", "ox"), P(None, None, "oy", "ox")),
        check_vma=False,
    )
```

```python
import jax
import jax.numpy as jnp
from jax import lax
from jax.sharding import PartitionSpec as P
from jax.experimental import pallas as pl
from jax.experimental.pallas import tpu as pltpu

H = 2
STEPS = 8
WIDE = 8
LANES = 384
HIGH = lax.Precision.HIGHEST


def with_halo(cells, sides, width, closed):
    for axis, dim in sides:
        count = lax.axis_size(axis)
        ends = count if closed else count - 1
        head = lax.slice_in_dim(cells, 0, width, axis=dim)
        tail = lax.slice_in_dim(cells, cells.shape[dim] - width, cells.shape[dim], axis=dim)
        cells = jnp.concatenate(
            [
                lax.ppermute(tail, axis, [(i, (i + 1) % count) for i in range(ends)]),
                cells,
                lax.ppermute(head, axis, [((i + 1) % count, i) for i in range(ends)]),
            ],
            axis=dim,
        )
    return cells


def exchange(blocks, flips):
    rows_n = lax.axis_size("oy")
    cols_n = lax.axis_size("ox")
    on_top = lax.axis_index("oy") == rows_n - 1
    sizes = [b.shape[0] for b in blocks]
    sign = jnp.concatenate(
        [jnp.full((n,), -1.0 if neg else 1.0, jnp.float32) for n, neg in zip(sizes, flips)]
    )[:, None, None]
    tops = jnp.concatenate([b[:, -WIDE:, :] for b in blocks], axis=0)
    bots = jnp.concatenate([b[:, :WIDE, :] for b in blocks], axis=0)
    south = lax.ppermute(tops, "oy", [(i, i + 1) for i in range(rows_n - 1)])
    north = lax.ppermute(bots, "oy", [(i + 1, i) for i in range(rows_n - 1)])
    top_row = (rows_n - 1) * cols_n
    fold = lax.ppermute(
        tops,
        ("oy", "ox"),
        [(top_row + (cols_n // 2 - j) % cols_n, top_row + j) for j in range(cols_n)],
    )
    north = jnp.where(on_top, fold[:, ::-1, ::-1] * sign, north)
    easts = jnp.concatenate(
        [jnp.concatenate([b[..., -WIDE:] for b in blocks], axis=0), north[..., -WIDE:], south[..., -WIDE:]],
        axis=1,
    )
    wests = jnp.concatenate(
        [jnp.concatenate([b[..., :WIDE] for b in blocks], axis=0), north[..., :WIDE], south[..., :WIDE]],
        axis=1,
    )
    from_w = lax.ppermute(easts, "ox", [(i, (i + 1) % cols_n) for i in range(cols_n)])
    from_e = lax.ppermute(wests, "ox", [((i + 1) % cols_n, i) for i in range(cols_n)])
    return north, south, (from_e, from_w)


def lane_tile(sides, cols):
    from_e, from_w = sides
    gap = jnp.zeros(from_e.shape[:-1] + (LANES - cols - 2 * WIDE,), jnp.float32)
    return jnp.concatenate([from_e, gap, from_w], axis=-1)


def stencil_kernel(tr_ref, u_ref, v_ref, m_ref, f_ref, hn_ref, hs_ref, hc_ref, fn_ref, fs_ref, fc_ref,
                   o_ref, buf, uu, vv, mm, ff, cw, ce, cs, cn, cc, m8, mf):
    nt, nk, orows, ocols = tr_ref.shape
    _, planes, rows, lanes = buf.shape

    def place(dst, own, at):
        dst[:orows, :ocols] = own
        dst[orows:orows + WIDE, :ocols] = hn_ref[at]
        dst[orows + WIDE:, :ocols] = hs_ref[at]
        dst[:, ocols:] = hc_ref[at]

    for p in range(planes):
        place(buf.at[0, p], tr_ref[p // nk, p % nk], p)

    for k in range(nk):
        place(uu.at[k], u_ref[k].astype(jnp.float32), planes + k)
        place(vv.at[k], v_ref[k].astype(jnp.float32), planes + nk + k)
    place(mm, m_ref[...].astype(jnp.float32), planes + 2 * nk)
    for t in range(nt):
        ff[t, :orows, :ocols] = f_ref[t]
        ff[t, orows:orows + WIDE, :ocols] = fn_ref[t]
        ff[t, orows + WIDE:, :ocols] = fs_ref[t]
        ff[t, :, ocols:] = fc_ref[t]

    mask = mm[...]
    m8[...] = mask * 0.08
    for t in range(nt):
        mf[t] = mask * ff[t]

    def coef(k, carry):
        u = uu[k]
        v = vv[k]
        up = jnp.maximum(u, 0.0)
        um = jnp.minimum(u, 0.0)
        vp = jnp.maximum(v, 0.0)
        vm = jnp.minimum(v, 0.0)
        cw[k] = mask * (up + 0.08)
        ce[k] = mask * (0.08 - um)
        cs[k] = mask * (vp + 0.08)
        cn[k] = mask * (0.08 - vm)
        cc[k] = mask * ((um - up) + (vm - vp) - 0.48)
        return carry

    for k in range(nk):
        coef(k, 0)

    strips = rows // 8
    first_row = lax.broadcasted_iota(jnp.int32, (8, lanes), 0) == 0
    last_row = lax.broadcasted_iota(jnp.int32, (8, lanes), 0) == 7

    def plane(src, dst, k, above, below, forced):
        for i in range(strips):
            at = pl.ds(i * 8, 8)
            before = pl.ds((i - 1) % strips * 8, 8)
            after = pl.ds((i + 1) % strips * 8, 8)
            c_w = cw[k, at, :]
            c_e = ce[k, at, :]
            c_s = cs[k, at, :]
            c_n = cn[k, at, :]
            c_c = cc[k, at, :]
            c_8 = m8[at, :]
            for t in range(nt):
                p = t * nk + k
                cur = buf[src, p, at, :]
                south = jnp.where(first_row, pltpu.roll(buf[src, p, before, :], 1, 0), pltpu.roll(cur, 1, 0))
                north = jnp.where(last_row, pltpu.roll(buf[src, p, after, :], 7, 0), pltpu.roll(cur, 7, 0))
                west = pltpu.roll(cur, 1, 1)
                east = pltpu.roll(cur, lanes - 1, 1)
                up = cur if above is None else buf[src, t * nk + above, at, :]
                down = cur if below is None else buf[src, t * nk + below, at, :]
                tend = c_w * west + c_e * east + c_s * south + c_n * north + c_c * cur
                tend = tend + c_8 * (up + down)
                if forced:
                    tend = tend + mf[t, at, :]
                buf[dst, p, at, :] = cur + tend

    def step(i, carry):
        for src in (0, 1):
            dst = 1 - src
            for k in range(nk):
                plane(src, dst, k, k - 1 if k > 0 else None, k + 1 if k < nk - 1 else None, k == 0)
        return carry

    lax.fori_loop(0, STEPS // 2, step, 0)

    for p in range(planes):
        o_ref[p // nk, p % nk] = buf[STEPS % 2, p, :orows, :ocols]


def evolve(tracers, u_vel, v_vel, land_mask, forcing, halo, f_halo):
    nt, nk, orows, ocols = tracers.shape
    plane = (orows + 2 * WIDE, LANES)
    vm = lambda *shape: pltpu.VMEM(shape, jnp.float32)
    return pl.pallas_call(
        stencil_kernel,
        out_shape=jax.ShapeDtypeStruct(tracers.shape, jnp.float32),
        scratch_shapes=[
            vm(2, nt * nk, *plane),
            vm(nk, *plane),
            vm(nk, *plane),
            vm(*plane),
            vm(nt, *plane),
            vm(nk, *plane),
            vm(nk, *plane),
            vm(nk, *plane),
            vm(nk, *plane),
            vm(nk, *plane),
            vm(*plane),
            vm(nt, *plane),
        ],
        compiler_params=pltpu.CompilerParams(vmem_limit_bytes=62 * 1024 * 1024),
    )(tracers, u_vel, v_vel, land_mask, forcing, *halo, *f_halo)


def atmosphere_block(atm_flux):
    cols_n = lax.axis_size("ox")
    rows_n = lax.axis_size("oy")
    width = atm_flux.shape[2] // cols_n
    nf, lat = atm_flux.shape[:2]
    body = jnp.roll(atm_flux, H, axis=2).reshape(nf, lat, cols_n, width)
    tail = jnp.roll(atm_flux, H - width, axis=2).reshape(nf, lat, cols_n, width)[..., : 2 * H]
    pieces = jnp.concatenate([body, tail], axis=3)
    got = lax.all_to_all(pieces, "ox", split_axis=2, concat_axis=1, tiled=True)
    own = got.reshape(nf, -1, width + 2 * H)
    below = lax.ppermute(own[:, -H:], "oy", [(i, i + 1) for i in range(rows_n - 1)])
    above = lax.ppermute(own[:, :H], "oy", [(i + 1, i) for i in range(rows_n - 1)])
    return jnp.concatenate([below, own, above], axis=1)


def remap(padded, remap_index, remap_weight):
    nf, arows, acols = padded.shape
    kk, orows, ocols = remap_index.shape
    base_r = jnp.arange(orows, dtype=jnp.int32) * (arows - 2 * H - 1) // (orows - 1) + H
    base_c = jnp.arange(ocols, dtype=jnp.int32) * (acols - 2 * H - 1) // (ocols - 1) + H
    offs = jnp.arange(2 * H + 1, dtype=jnp.int32) - H
    pick_c = (
        jnp.arange(acols, dtype=jnp.int32)[:, None, None]
        == (base_c[None, None, :] + offs[None, :, None])
    ).astype(jnp.float32).reshape(acols, -1)
    lifted = jnp.einsum("fab,bq->faq", padded, pick_c, precision=HIGH)
    lifted = lifted.reshape(nf, arows, 2 * H + 1, ocols)
    window = lifted[:, base_r[None, :] + offs[:, None]]
    row_of = remap_index // acols - base_r[None, :, None] + H
    col_of = remap_index % acols - base_c[None, None, :] + H
    inside = (row_of >= 0) & (row_of <= 2 * H) & (col_of >= 0) & (col_of <= 2 * H)
    slot = jnp.where(inside, row_of * (2 * H + 1) + col_of, -1)
    slots = jnp.arange((2 * H + 1) ** 2, dtype=jnp.int32)
    wsum = jnp.sum(
        jnp.where(slot[:, None] == slots[None, :, None, None], remap_weight[:, None], 0.0),
        axis=0,
    ).reshape(2 * H + 1, 2 * H + 1, orows, ocols)
    fast = jnp.sum(window * wsum.transpose(0, 2, 1, 3)[None], axis=(1, 3))
    missed = jnp.logical_not(jnp.all(inside))

    def general():
        flat = padded.reshape(nf, -1)
        total = jnp.zeros((nf,) + remap_index.shape[1:], jnp.float32)
        for source in range(kk):
            picked = jnp.take(flat, remap_index[source], axis=1)
            total = total + remap_weight[source][None] * picked
        return total

    return lax.cond(missed, general, lambda: fast)


def on_device(atm_flux, remap_index, remap_weight, coupling, land_mask, tracers, u_vel, v_vel):
    fields = [
        tracers.reshape((-1,) + tracers.shape[2:]),
        u_vel.astype(jnp.float32),
        v_vel.astype(jnp.float32),
        land_mask.astype(jnp.float32)[None],
    ]
    halo = exchange(fields, [False, True, True, False])

    padded = atmosphere_block(atm_flux)
    halo, padded = lax.optimization_barrier((halo, padded))
    ocean_flux = remap(padded, remap_index, remap_weight)
    forcing = jnp.sum(coupling[:, :, None, None] * ocean_flux[None], axis=1)
    sides, forcing = lax.optimization_barrier((halo[2], forcing))
    halo = (halo[0], halo[1], lane_tile(sides, tracers.shape[-1]))
    f_halo = exchange([forcing], [False])
    f_halo = (f_halo[0], f_halo[1], lane_tile(f_halo[2], tracers.shape[-1]))
    final = evolve(tracers, u_vel, v_vel, land_mask, forcing, halo, f_halo)
    return (ocean_flux, final)


def solution(mesh):
    placed = (
        P(None, ("oy", "ox"), None),
        P(None, "oy", "ox"),
        P(None, "oy", "ox"),
        P(),
        P("oy", "ox"),
        P(None, None, "oy", "ox"),
        P(None, "oy", "ox"),
        P(None, "oy", "ox"),
    )
    return jax.shard_map(
        on_device,
        mesh=mesh,
        in_specs=placed,
        out_specs=(P(None, "oy", "ox"), P(None, None, "oy", "ox")),
        check_vma=False,
    )
```

```python
import jax
import jax.numpy as jnp
from jax import lax
from jax.sharding import PartitionSpec as P
from jax.experimental import pallas as pl
from jax.experimental.pallas import tpu as pltpu

H = 2
STEPS = 8
WIDE = 8
LANES = 384
HIGH = lax.Precision.HIGHEST


def with_halo(cells, sides, width, closed):
    for axis, dim in sides:
        count = lax.axis_size(axis)
        ends = count if closed else count - 1
        head = lax.slice_in_dim(cells, 0, width, axis=dim)
        tail = lax.slice_in_dim(cells, cells.shape[dim] - width, cells.shape[dim], axis=dim)
        cells = jnp.concatenate(
            [
                lax.ppermute(tail, axis, [(i, (i + 1) % count) for i in range(ends)]),
                cells,
                lax.ppermute(head, axis, [((i + 1) % count, i) for i in range(ends)]),
            ],
            axis=dim,
        )
    return cells


def exchange(blocks, flips):
    rows_n = lax.axis_size("oy")
    cols_n = lax.axis_size("ox")
    on_top = lax.axis_index("oy") == rows_n - 1
    sizes = [b.shape[0] for b in blocks]
    sign = jnp.concatenate(
        [jnp.full((n,), -1.0 if neg else 1.0, jnp.float32) for n, neg in zip(sizes, flips)]
    )[:, None, None]
    tops = jnp.concatenate([b[:, -WIDE:, :] for b in blocks], axis=0)
    bots = jnp.concatenate([b[:, :WIDE, :] for b in blocks], axis=0)
    south = lax.ppermute(tops, "oy", [(i, i + 1) for i in range(rows_n - 1)])
    north = lax.ppermute(bots, "oy", [(i + 1, i) for i in range(rows_n - 1)])
    top_row = (rows_n - 1) * cols_n
    fold = lax.ppermute(
        tops,
        ("oy", "ox"),
        [(top_row + (cols_n // 2 - j) % cols_n, top_row + j) for j in range(cols_n)],
    )
    north = jnp.where(on_top, fold[:, ::-1, ::-1] * sign, north)
    easts = jnp.concatenate(
        [jnp.concatenate([b[..., -WIDE:] for b in blocks], axis=0), north[..., -WIDE:], south[..., -WIDE:]],
        axis=1,
    )
    wests = jnp.concatenate(
        [jnp.concatenate([b[..., :WIDE] for b in blocks], axis=0), north[..., :WIDE], south[..., :WIDE]],
        axis=1,
    )
    from_w = lax.ppermute(easts, "ox", [(i, (i + 1) % cols_n) for i in range(cols_n)])
    from_e = lax.ppermute(wests, "ox", [((i + 1) % cols_n, i) for i in range(cols_n)])
    return north, south, (from_e, from_w)


def lane_tile(sides, cols):
    from_e, from_w = sides
    gap = jnp.zeros(from_e.shape[:-1] + (LANES - cols - 2 * WIDE,), jnp.float32)
    return jnp.concatenate([from_e, gap, from_w], axis=-1)


def stencil_kernel(tr_ref, u_ref, v_ref, m_ref, f_ref, hn_ref, hs_ref, hc_ref, fn_ref, fs_ref, fc_ref,
                   o_ref, buf, uu, vv, mm, ff, cw, ce, cs, cn, cc, m8, mf):
    nt, nk, orows, ocols = tr_ref.shape
    _, planes, rows, lanes = buf.shape

    def place(dst, own, at):
        dst[:orows, :ocols] = own
        dst[orows:orows + WIDE, :ocols] = hn_ref[at]
        dst[orows + WIDE:, :ocols] = hs_ref[at]
        dst[:, ocols:] = hc_ref[at]

    for p in range(planes):
        place(buf.at[0, p], tr_ref[p // nk, p % nk], p)

    for k in range(nk):
        place(uu.at[k], u_ref[k].astype(jnp.float32), planes + k)
        place(vv.at[k], v_ref[k].astype(jnp.float32), planes + nk + k)
    place(mm, m_ref[...].astype(jnp.float32), planes + 2 * nk)
    for t in range(nt):
        ff[t, :orows, :ocols] = f_ref[t]
        ff[t, orows:orows + WIDE, :ocols] = fn_ref[t]
        ff[t, orows + WIDE:, :ocols] = fs_ref[t]
        ff[t, :, ocols:] = fc_ref[t]

    mask = mm[...]
    m8[...] = mask * 0.08
    for t in range(nt):
        mf[t] = mask * ff[t]

    def coef(k, carry):
        u = uu[k]
        v = vv[k]
        up = jnp.maximum(u, 0.0)
        um = jnp.minimum(u, 0.0)
        vp = jnp.maximum(v, 0.0)
        vm = jnp.minimum(v, 0.0)
        cw[k] = mask * (up + 0.08)
        ce[k] = mask * (0.08 - um)
        cs[k] = mask * (vp + 0.08)
        cn[k] = mask * (0.08 - vm)
        cc[k] = mask * ((um - up) + (vm - vp) - 0.48)
        return carry

    for k in range(nk):
        coef(k, 0)

    strips = rows // 8
    first_row = lax.broadcasted_iota(jnp.int32, (8, lanes), 0) == 0
    last_row = lax.broadcasted_iota(jnp.int32, (8, lanes), 0) == 7

    def plane(src, dst, k, above, below, forced, final=False):
        for i in range(orows // 8 if final else strips):
            at = pl.ds(i * 8, 8)
            before = pl.ds((i - 1) % strips * 8, 8)
            after = pl.ds((i + 1) % strips * 8, 8)
            c_w = cw[k, at, :]
            c_e = ce[k, at, :]
            c_s = cs[k, at, :]
            c_n = cn[k, at, :]
            c_c = cc[k, at, :]
            c_8 = m8[at, :]
            for t in range(nt):
                p = t * nk + k
                cur = buf[src, p, at, :]
                south = jnp.where(first_row, pltpu.roll(buf[src, p, before, :], 1, 0), pltpu.roll(cur, 1, 0))
                north = jnp.where(last_row, pltpu.roll(buf[src, p, after, :], 7, 0), pltpu.roll(cur, 7, 0))
                west = pltpu.roll(cur, 1, 1)
                east = pltpu.roll(cur, lanes - 1, 1)
                up = cur if above is None else buf[src, t * nk + above, at, :]
                down = cur if below is None else buf[src, t * nk + below, at, :]
                tend = c_w * west + c_e * east + c_s * south + c_n * north + c_c * cur
                tend = tend + c_8 * (up + down)
                if forced:
                    tend = tend + mf[t, at, :]
                if final:
                    o_ref[t, k, at, :] = (cur + tend)[:, :ocols]
                else:
                    buf[dst, p, at, :] = cur + tend

    def step(i, carry):
        for src in (0, 1):
            dst = 1 - src
            for k in range(nk):
                plane(src, dst, k, k - 1 if k > 0 else None, k + 1 if k < nk - 1 else None, k == 0)
        return carry

    lax.fori_loop(0, STEPS // 2 - 1, step, 0)
    for k in range(nk):
        plane(0, 1, k, k - 1 if k > 0 else None, k + 1 if k < nk - 1 else None, k == 0)
    for k in range(nk):
        plane(1, None, k, k - 1 if k > 0 else None, k + 1 if k < nk - 1 else None, k == 0, True)


def evolve(tracers, u_vel, v_vel, land_mask, forcing, halo, f_halo):
    nt, nk, orows, ocols = tracers.shape
    plane = (orows + 2 * WIDE, LANES)
    vm = lambda *shape: pltpu.VMEM(shape, jnp.float32)
    return pl.pallas_call(
        stencil_kernel,
        out_shape=jax.ShapeDtypeStruct(tracers.shape, jnp.float32),
        scratch_shapes=[
            vm(2, nt * nk, *plane),
            vm(nk, *plane),
            vm(nk, *plane),
            vm(*plane),
            vm(nt, *plane),
            vm(nk, *plane),
            vm(nk, *plane),
            vm(nk, *plane),
            vm(nk, *plane),
            vm(nk, *plane),
            vm(*plane),
            vm(nt, *plane),
        ],
        compiler_params=pltpu.CompilerParams(vmem_limit_bytes=62 * 1024 * 1024),
    )(tracers, u_vel, v_vel, land_mask, forcing, *halo, *f_halo)


def atmosphere_block(atm_flux):
    cols_n = lax.axis_size("ox")
    rows_n = lax.axis_size("oy")
    width = atm_flux.shape[2] // cols_n
    nf, lat = atm_flux.shape[:2]
    body = jnp.roll(atm_flux, H, axis=2).reshape(nf, lat, cols_n, width)
    tail = jnp.roll(atm_flux, H - width, axis=2).reshape(nf, lat, cols_n, width)[..., : 2 * H]
    pieces = jnp.concatenate([body, tail], axis=3)
    got = lax.all_to_all(pieces, "ox", split_axis=2, concat_axis=1, tiled=True)
    own = got.reshape(nf, -1, width + 2 * H)
    below = lax.ppermute(own[:, -H:], "oy", [(i, i + 1) for i in range(rows_n - 1)])
    above = lax.ppermute(own[:, :H], "oy", [(i + 1, i) for i in range(rows_n - 1)])
    return jnp.concatenate([below, own, above], axis=1)


def remap(padded, remap_index, remap_weight):
    nf, arows, acols = padded.shape
    kk, orows, ocols = remap_index.shape
    base_r = jnp.arange(orows, dtype=jnp.int32) * (arows - 2 * H - 1) // (orows - 1) + H
    base_c = jnp.arange(ocols, dtype=jnp.int32) * (acols - 2 * H - 1) // (ocols - 1) + H
    offs = jnp.arange(2 * H + 1, dtype=jnp.int32) - H
    pick_c = (
        jnp.arange(acols, dtype=jnp.int32)[:, None, None]
        == (base_c[None, None, :] + offs[None, :, None])
    ).astype(jnp.float32).reshape(acols, -1)
    lifted = jnp.einsum("fab,bq->faq", padded, pick_c, precision=HIGH)
    lifted = lifted.reshape(nf, arows, 2 * H + 1, ocols)
    window = lifted[:, base_r[None, :] + offs[:, None]]
    row_of = remap_index // acols - base_r[None, :, None] + H
    col_of = remap_index % acols - base_c[None, None, :] + H
    inside = (row_of >= 0) & (row_of <= 2 * H) & (col_of >= 0) & (col_of <= 2 * H)
    slot = jnp.where(inside, row_of * (2 * H + 1) + col_of, -1)
    slots = jnp.arange((2 * H + 1) ** 2, dtype=jnp.int32)
    wsum = jnp.sum(
        jnp.where(slot[:, None] == slots[None, :, None, None], remap_weight[:, None], 0.0),
        axis=0,
    ).reshape(2 * H + 1, 2 * H + 1, orows, ocols)
    fast = jnp.sum(window * wsum.transpose(0, 2, 1, 3)[None], axis=(1, 3))
    missed = jnp.logical_not(jnp.all(inside))

    def general():
        flat = padded.reshape(nf, -1)
        total = jnp.zeros((nf,) + remap_index.shape[1:], jnp.float32)
        for source in range(kk):
            picked = jnp.take(flat, remap_index[source], axis=1)
            total = total + remap_weight[source][None] * picked
        return total

    return lax.cond(missed, general, lambda: fast)


def on_device(atm_flux, remap_index, remap_weight, coupling, land_mask, tracers, u_vel, v_vel):
    fields = [
        tracers.reshape((-1,) + tracers.shape[2:]),
        u_vel.astype(jnp.float32),
        v_vel.astype(jnp.float32),
        land_mask.astype(jnp.float32)[None],
    ]
    halo = exchange(fields, [False, True, True, False])

    padded = atmosphere_block(atm_flux)
    halo, padded = lax.optimization_barrier((halo, padded))
    ocean_flux = remap(padded, remap_index, remap_weight)
    forcing = jnp.sum(coupling[:, :, None, None] * ocean_flux[None], axis=1)
    sides, forcing = lax.optimization_barrier((halo[2], forcing))
    halo = (halo[0], halo[1], lane_tile(sides, tracers.shape[-1]))
    f_halo = exchange([forcing], [False])
    f_halo = (f_halo[0], f_halo[1], lane_tile(f_halo[2], tracers.shape[-1]))
    final = evolve(tracers, u_vel, v_vel, land_mask, forcing, halo, f_halo)
    return (ocean_flux, final)


def solution(mesh):
    placed = (
        P(None, ("oy", "ox"), None),
        P(None, "oy", "ox"),
        P(None, "oy", "ox"),
        P(),
        P("oy", "ox"),
        P(None, None, "oy", "ox"),
        P(None, "oy", "ox"),
        P(None, "oy", "ox"),
    )
    return jax.shard_map(
        on_device,
        mesh=mesh,
        in_specs=placed,
        out_specs=(P(None, "oy", "ox"), P(None, None, "oy", "ox")),
        check_vma=False,
    )
```
